32 devices in a mesh: slab: 8 (over z, y), col: 4 (over x, core).
Axes of the slice: x: 2, y: 2, z: 4, core: 2. Of those that a mesh axis runs over, the one named last changes fastest.
Arguments:
- rhs_force: float32 [3, 32, 32, 384], P(None, 'slab', 'col'), may hold values from -33 to 33
- integrity: bfloat16 [61, 32, 32, 384], P(None, 'slab', 'col'), may hold values from 0 to 1
- contact: int32 [32, 32, 384], P('slab', 'col'), may hold values 0 or 1
- coarse_inverse: float32 [768, 768], P(('slab', 'col')), may hold values from 0 to 6, as said below
Outputs:
- displacement: float32 [3, 32, 32, 384], P(None, 'slab', 'col')
- residual: float32 [3, 32, 32, 384], P(None, 'slab', 'col')
The draws below stay inside these ranges and needn't reach their ends.
Inputs may be any that keep to these rules, and one draw needn't show every extreme that they name: `coarse_inverse`: symmetric and positive definite, with no negative entry.
All inputs are finite; a program needn't handle non-finite values. No bound on the sum of `contact` on one device may be relied on, other than what follows from the above.
Results may differ from the reference program's by a relative error of at most 0.0007.
Values may be sent and summed in bfloat16 or wider, within the bound.
No kernel may reach another device: no remote copies, remote signals or barrier semaphores. Data moves between devices by JAX's collectives and lax.ppermute only.
A program may use at most 128 MiB of HBM per device.

```python
import jax
import jax.numpy as jnp
import numpy as np
from jax import lax

CX = 4
CY = 8
NZ = 384
BONDS = 61
AGG = 8
ITERS = 2
NX = 32
NY = 32
COARSE = 768


def draw_rhs_force(key, part):
    key_one = jax.random.fold_in(key, 0)
    row_index = jnp.arange(NX, dtype=jnp.float32)
    rise_factor = jnp.exp(jnp.log(3.0) * row_index / (NX - 1)).reshape(1, NX, 1, 1)
    col_index = jnp.arange(NY, dtype=jnp.float32)
    wave_part = (0.5 + 0.4 * jnp.cos(2.0 * jnp.pi * col_index / NY)).reshape(1, 1, NY, 1)
    normal_part = jnp.clip(jax.random.normal(key_one, (3, NX, NY, NZ), jnp.float32), -6.0, 6.0)
    return rise_factor * (wave_part + normal_part)


def draw_coarse_inverse(key, part):
    key_one, key_two = jax.random.split(key)
    raw_entries = jax.random.uniform(key_one, (COARSE, COARSE), jnp.float32, 0.0, 2.0 / COARSE)
    symmetric = 0.5 * (raw_entries + raw_entries.T)
    identity = jnp.eye(COARSE, dtype=jnp.float32)
    diagonal = jax.random.uniform(key_two, (COARSE,), jnp.float32, 2.2, 4.0)
    return symmetric * (1.0 - identity) + identity * diagonal[None, :]


def touch_ends(entries, key, smallest, top_value):
    place = [jax.random.randint(jax.random.fold_in(key, axis), (), 0, length) for axis, length in enumerate(entries.shape)]
    main_axis = entries.shape.index(max(entries.shape))
    next_to = place[:main_axis] + [(place[main_axis] + 1) % entries.shape[main_axis]] + place[main_axis + 1:]
    return entries.at[tuple(place)].set(smallest).at[tuple(next_to)].set(top_value)


def steps_of(rng, dims, shards, smallest, top_value):
    loudness, own = 1.0, jax.random.fold_in(rng, 6)
    for position, parts in shards:
        steps = jnp.exp(jax.random.uniform(jax.random.fold_in(own, position), (parts,), jnp.float32, smallest / len(shards), top_value / len(shards)))
        loudness = loudness * jnp.repeat(steps, dims[position] // parts).reshape([-1 if axis == position else 1 for axis in range(len(dims))])
    return loudness


def setup_inputs(seed: int = 0) -> dict:
    splits = jax.random.split(jax.random.key(seed), 5)
    rhs_force = draw_rhs_force(jax.random.fold_in(splits[4], 71), 0)
    integrity = jnp.clip(1.0 * jax.random.uniform(splits[1], (BONDS, NX, NY, NZ), jnp.float32) ** steps_of(splits[1], (BONDS, NX, NY, NZ), ((1, 8), (2, 4)), -0.2, 0.2), 0.0, 1.0).astype(jnp.bfloat16)
    contact = touch_ends((jax.random.randint(splits[2], (NX, NY, NZ), 0, 2) < 1).astype(jnp.int32), jax.random.fold_in(splits[2], 1), 0, 1)
    coarse_inverse = draw_coarse_inverse(jax.random.fold_in(splits[4], 71), 0)
    return dict(rhs_force=rhs_force, integrity=integrity, contact=contact, coarse_inverse=coarse_inverse)


STIFFNESS = 0.6
PENALTY = 2.0
FOUNDATION = 1.0

def bond_list():
    listed = []
    for shift_x in range(-3, 4):
        for shift_y in range(-3, 4):
            for shift_z in range(-3, 4):
                radius = shift_x * shift_x + shift_y * shift_y + shift_z * shift_z
                if 0 < radius <= 9 and (shift_x, shift_y, shift_z) > (0, 0, 0):
                    listed.append((shift_x, shift_y, shift_z))
    return listed

def bond_tables():
    offsets = np.array(bond_list(), dtype=np.int32)
    lengths = np.sqrt(np.sum(offsets * offsets, axis=1).astype(np.float32)).astype(np.float32)
    unit_dirs = (offsets.astype(np.float32) / lengths[:, None]).astype(np.float32)
    weights = (np.float32(STIFFNESS) / lengths).astype(np.float32)
    nearest = (lengths < 1.5).astype(np.float32)
    return (offsets, unit_dirs, weights, nearest)

def pad_vector(vector):
    return jnp.pad(vector, ((0, 0), (3, 3), (3, 3), (3, 3)))

def reference(rhs_force, integrity, contact, coarse_inverse):
    grid_shape = (NX, NY, NZ)
    offsets, unit_dirs, weights, nearest = bond_tables()
    bond_data = (integrity, jnp.asarray(offsets), jnp.asarray(unit_dirs), jnp.asarray(weights), jnp.asarray(nearest))
    contact_pad = jnp.pad(contact.astype(jnp.float32), 3)
    inside_pad = jnp.pad(jnp.ones(grid_shape, jnp.float32), 3)
    near_contact = contact_pad[3:-3, 3:-3, 3:-3]
    zero_index = jnp.zeros((), jnp.int32)

    def coefficients(intact, offset, weight, nearness):
        start_at = (offset + 3).astype(jnp.int32)
        far_contact = lax.dynamic_slice(contact_pad, (start_at[0], start_at[1], start_at[2]), grid_shape)
        far_inside = lax.dynamic_slice(inside_pad, (start_at[0], start_at[1], start_at[2]), grid_shape)
        forward = far_inside * (weight * intact + nearness * PENALTY * near_contact * far_contact * (1.0 - intact))
        back_at = (3 - offset).astype(jnp.int32)
        backward = lax.dynamic_slice(jnp.pad(forward, 3), (back_at[0], back_at[1], back_at[2]), grid_shape)
        return (forward, backward)

    def diagonal_step(summed, bond_slice):
        intact, offset, unit_dir, weight, nearness = bond_slice
        forward, backward = coefficients(intact.astype(jnp.float32), offset, weight, nearness)
        unit_col = unit_dir.reshape(3, 1, 1, 1)
        return (summed + unit_col * unit_col * (forward + backward)[None], None)
    diagonal, unused = lax.scan(diagonal_step, FOUNDATION * jnp.ones((3,) + grid_shape, jnp.float32), bond_data)

    def operator(vector):
        padded = pad_vector(vector)

        def bond_step(summed, bond_slice):
            intact, offset, unit_dir, weight, nearness = bond_slice
            forward, backward = coefficients(intact.astype(jnp.float32), offset, weight, nearness)
            start_at = (offset + 3).astype(jnp.int32)
            back_at = (3 - offset).astype(jnp.int32)
            ahead_vec = lax.dynamic_slice(padded, (zero_index, start_at[0], start_at[1], start_at[2]), (3,) + grid_shape)
            behind = lax.dynamic_slice(padded, (zero_index, back_at[0], back_at[1], back_at[2]), (3,) + grid_shape)
            unit_col = unit_dir.reshape(3, 1, 1, 1)
            stretch = forward * lax.optimization_barrier(jnp.sum(unit_col * (vector - ahead_vec), axis=0))
            stretch = stretch + backward * lax.optimization_barrier(jnp.sum(unit_col * (vector - behind), axis=0))
            return (summed + unit_col * stretch[None], None)
        summed, unused_out = lax.scan(bond_step, FOUNDATION * vector, bond_data)
        return summed
    slab_count = NX // CX
    columns = NY // CY
    agg_depth = NZ // AGG
    agg_cells = CX * CY * agg_depth

    def coarse_means(vector):
        blocks = vector.reshape(3, slab_count, CX, columns, CY, AGG, agg_depth)
        return (lax.optimization_barrier(jnp.sum(blocks, axis=(2, 4, 6))) / agg_cells).transpose(1, 2, 3, 0).reshape(COARSE)

    def precondition(vector):
        solved = jnp.dot(coarse_inverse, coarse_means(vector), precision=lax.Precision.HIGHEST)
        spread = solved.reshape(slab_count, columns, AGG, 3).transpose(3, 0, 1, 2)[:, :, None, :, None, :, None]
        spread = jnp.broadcast_to(spread, (3, slab_count, CX, columns, CY, AGG, agg_depth)).reshape((3,) + grid_shape)
        return vector / diagonal + spread
    displacement = jnp.zeros_like(rhs_force)
    residual = rhs_force
    precond_r = precondition(residual)
    rz_now = jnp.sum(residual * precond_r)
    direction = precond_r
    for iteration in range(ITERS):
        image_vec = operator(direction)
        step_size = rz_now / jnp.sum(direction * image_vec)
        displacement = displacement + step_size * direction
        residual = residual - step_size * image_vec
        precond_r = precondition(residual)
        fresh_rz = jnp.sum(residual * precond_r)
        direction = precond_r + fresh_rz / rz_now * direction
        rz_now = fresh_rz
    return (displacement, residual)
```

```python
import jax
import jax.numpy as jnp
import numpy as np
from jax import lax
from jax.sharding import PartitionSpec as P

ITERS = 2


STIFFNESS = 0.6
PENALTY = 2.0
FOUNDATION = 1.0


def with_halo(x, sides, width, low=True, high=True):
    for axis, dim in sides:
        count, length = (lax.axis_size(axis), x.shape[dim])
        up = [(i, (i + 1) % count) for i in range(count - 1)]
        down = [(j, i) for i, j in up]
        last = lax.slice_in_dim(x, length - width, length, axis=dim)
        first = lax.slice_in_dim(x, 0, width, axis=dim)
        parts = [x]
        if low:
            parts.insert(0, lax.ppermute(last, axis, up))
        if high:
            parts.append(lax.ppermute(first, axis, down))
        x = jnp.concatenate(parts, axis=dim)
    return x


def device_rows(vector, axes):
    count = 1
    for axis in axes:
        count = count * lax.axis_size(axis)
    tiled = jnp.broadcast_to(vector[None], (count,) + vector.shape)
    return lax.all_to_all(tiled, axes, 0, 0, tiled=True)


def bond_list():
    listed = []
    for shift_x in range(-3, 4):
        for shift_y in range(-3, 4):
            for shift_z in range(-3, 4):
                radius = shift_x * shift_x + shift_y * shift_y + shift_z * shift_z
                if 0 < radius <= 9 and (shift_x, shift_y, shift_z) > (0, 0, 0):
                    listed.append((shift_x, shift_y, shift_z))
    return listed


def bond_tables():
    offsets = np.array(bond_list(), dtype=np.int32)
    lengths = np.sqrt(np.sum(offsets * offsets, axis=1).astype(np.float32)).astype(np.float32)
    unit_dirs = (offsets.astype(np.float32) / lengths[:, None]).astype(np.float32)
    weights = (np.float32(STIFFNESS) / lengths).astype(np.float32)
    nearest = (lengths < 1.5).astype(np.float32)
    return (offsets, unit_dirs, weights, nearest)


def rim_mask(count, whole, position):
    places = position * count + jnp.arange(count + 6, dtype=jnp.int32) - 3
    return ((places >= 0) & (places < whole)).astype(jnp.float32)


def window(array, shift_x, shift_y, shift_z, extent):
    return array[
        ...,
        3 + shift_x : 3 + shift_x + extent[0],
        3 + shift_y : 3 + shift_y + extent[1],
        3 + shift_z : 3 + shift_z + extent[2],
    ]


def pad_depth(array):
    return jnp.pad(array, [(0, 0)] * (array.ndim - 1) + [(3, 3)])


def on_device(rhs_force, integrity, contact, coarse_inverse):
    components, cells_x, cells_y, depth = rhs_force.shape
    bond_count = integrity.shape[0]
    aggregates = coarse_inverse.shape[0] // 3
    agg_depth = depth // aggregates
    agg_cells = cells_x * cells_y * agg_depth
    extent = (cells_x, cells_y, depth)
    offsets, unit_dirs, weights, nearest = bond_tables()
    slab_mask = rim_mask(cells_x, cells_x * lax.axis_size("slab"), lax.axis_index("slab"))
    col_mask = rim_mask(cells_y, cells_y * lax.axis_size("col"), lax.axis_index("col"))
    depth_mask = rim_mask(depth, depth, jnp.zeros((), jnp.int32))
    inside_pad = slab_mask[:, None, None] * col_mask[None, :, None] * depth_mask[None, None, :]

    def bond_shift(bond_index):
        return [int(entry) for entry in offsets[bond_index]]

    def heading_of(bond_index):
        return [float(unit_dirs[bond_index, component]) for component in range(3)]

    def rimmed(vector):
        return pad_depth(with_halo(vector, (("slab", 1), ("col", 2)), 3))

    lower_x = with_halo(integrity, (("slab", 1),), 3, high=False)
    spread = pad_depth(with_halo(lower_x, (("col", 2),), 3))
    contact_pad = pad_depth(
        with_halo(contact.astype(jnp.bfloat16), (("slab", 0), ("col", 1)), 3)
    ).astype(jnp.float32)
    near_contact = window(contact_pad, 0, 0, 0, extent)

    def bond_pair(bond_index):
        shift_x, shift_y, shift_z = bond_shift(bond_index)
        weight = float(weights[bond_index])
        level_pad = jnp.pad(spread[bond_index], ((0, 3), (0, 0), (0, 0)))
        intact = window(level_pad, 0, 0, 0, extent).astype(jnp.float32)
        prior = window(level_pad, -shift_x, -shift_y, -shift_z, extent).astype(jnp.float32)
        forward = weight * intact
        backward = weight * prior
        if nearest[bond_index] > 0.5:
            forward = forward + PENALTY * near_contact * window(
                contact_pad, shift_x, shift_y, shift_z, extent
            ) * (1.0 - intact)
            backward = backward + PENALTY * window(
                contact_pad, -shift_x, -shift_y, -shift_z, extent
            ) * near_contact * (1.0 - prior)
        forward = window(inside_pad, shift_x, shift_y, shift_z, extent) * forward
        return (forward, backward)

    diag_list = [jnp.full(extent, FOUNDATION, jnp.float32) for component in range(3)]
    for bond_index in range(bond_count):
        forward, backward = bond_pair(bond_index)
        heading = heading_of(bond_index)
        both_ends = forward + backward
        for component in range(3):
            diag_list[component] = (
                diag_list[component] + heading[component] * heading[component] * both_ends
            )
    diagonal = jnp.stack(diag_list)

    def operator(vector):
        padded = rimmed(vector)
        summed = [FOUNDATION * vector[component] for component in range(3)]
        for bond_index in range(bond_count):
            shift_x, shift_y, shift_z = bond_shift(bond_index)
            forward, backward = bond_pair(bond_index)
            heading = heading_of(bond_index)
            ahead_part = heading[0] * (
                vector[0] - window(padded[0], shift_x, shift_y, shift_z, extent)
            )
            behind_part = heading[0] * (
                vector[0] - window(padded[0], -shift_x, -shift_y, -shift_z, extent)
            )
            for component in range(1, 3):
                ahead_part = ahead_part + heading[component] * (
                    vector[component] - window(padded[component], shift_x, shift_y, shift_z, extent)
                )
                behind_part = behind_part + heading[component] * (
                    vector[component]
                    - window(padded[component], -shift_x, -shift_y, -shift_z, extent)
                )
            stretch = forward * ahead_part + backward * behind_part
            for component in range(3):
                summed[component] = summed[component] + heading[component] * stretch
        return jnp.stack(summed)

    def local_means(vector):
        blocks = vector.reshape(3, cells_x * cells_y, aggregates, agg_depth)
        return (jnp.sum(blocks, axis=(1, 3)) / agg_cells).T.reshape(3 * aggregates)

    def precondition(vector, coarse):
        solved = jnp.dot(coarse_inverse, coarse, precision=lax.Precision.HIGHEST)
        spread_back = solved.reshape(aggregates, 3).T[:, None, :, None]
        scaled = (vector / diagonal).reshape(
            3, cells_x * cells_y, aggregates, agg_depth
        ) + spread_back
        return scaled.reshape(vector.shape)

    every = ("slab", "col")

    def total(vector):
        return jnp.sum(device_rows(vector, every), axis=0)

    residual = rhs_force
    coarse_now = device_rows(local_means(residual), every).reshape(-1)
    direction = precondition(residual, coarse_now)
    image_vec = operator(direction)
    sums = device_rows(
        jnp.concatenate(
            [
                jnp.stack([jnp.sum(residual * direction), jnp.sum(direction * image_vec)]),
                local_means(image_vec),
            ]
        ),
        every,
    )
    rz_now = jnp.sum(sums[:, 0])
    step_size = rz_now / jnp.sum(sums[:, 1])
    image_means = sums[:, 2:].reshape(-1)
    displacement = step_size * direction
    residual = residual - step_size * image_vec
    for iteration in range(1, ITERS):
        coarse_now = coarse_now - step_size * image_means
        precond_r = precondition(residual, coarse_now)
        fresh_rz = total(jnp.sum(residual * precond_r)[None])[0]
        direction = precond_r + fresh_rz / rz_now * direction
        rz_now = fresh_rz
        image_vec = operator(direction)
        if iteration + 1 < ITERS:
            sums = device_rows(
                jnp.concatenate(
                    [jnp.sum(direction * image_vec)[None], local_means(image_vec)]
                ),
                every,
            )
            step_size = rz_now / jnp.sum(sums[:, 0])
            image_means = sums[:, 1:].reshape(-1)
        else:
            step_size = rz_now / total(jnp.sum(direction * image_vec)[None])[0]
        displacement = displacement + step_size * direction
        residual = residual - step_size * image_vec
    return (displacement, residual)


def solution(mesh):
    return jax.shard_map(
        on_device,
        mesh=mesh,
        in_specs=(
            P(None, "slab", "col", None),
            P(None, "slab", "col", None),
            P("slab", "col", None),
            P(("slab", "col"), None),
        ),
        out_specs=(P(None, "slab", "col", None), P(None, "slab", "col", None)),
        check_vma=False,
    )
```

```python
import jax
import jax.numpy as jnp
import numpy as np
from jax import lax
from jax.sharding import PartitionSpec as P

ITERS = 2


STIFFNESS = 0.6
PENALTY = 2.0
FOUNDATION = 1.0


def with_halo(x, sides, width, low=True, high=True):
    for axis, dim in sides:
        count, length = (lax.axis_size(axis), x.shape[dim])
        up = [(i, (i + 1) % count) for i in range(count - 1)]
        down = [(j, i) for i, j in up]
        last = lax.slice_in_dim(x, length - width, length, axis=dim)
        first = lax.slice_in_dim(x, 0, width, axis=dim)
        parts = [x]
        if low:
            parts.insert(0, lax.ppermute(last, axis, up))
        if high:
            parts.append(lax.ppermute(first, axis, down))
        x = jnp.concatenate(parts, axis=dim)
    return x


def device_rows(vector, axes):
    count = 1
    for axis in axes:
        count = count * lax.axis_size(axis)
    tiled = jnp.broadcast_to(vector[None], (count,) + vector.shape)
    return lax.all_to_all(tiled, axes, 0, 0, tiled=True)


def bond_list():
    listed = []
    for shift_x in range(-3, 4):
        for shift_y in range(-3, 4):
            for shift_z in range(-3, 4):
                radius = shift_x * shift_x + shift_y * shift_y + shift_z * shift_z
                if 0 < radius <= 9 and (shift_x, shift_y, shift_z) > (0, 0, 0):
                    listed.append((shift_x, shift_y, shift_z))
    return listed


def bond_tables():
    offsets = np.array(bond_list(), dtype=np.int32)
    lengths = np.sqrt(np.sum(offsets * offsets, axis=1).astype(np.float32)).astype(np.float32)
    unit_dirs = (offsets.astype(np.float32) / lengths[:, None]).astype(np.float32)
    weights = (np.float32(STIFFNESS) / lengths).astype(np.float32)
    nearest = (lengths < 1.5).astype(np.float32)
    return (offsets, unit_dirs, weights, nearest)


def rim_mask(count, whole, position):
    places = position * count + jnp.arange(count + 6, dtype=jnp.int32) - 3
    return ((places >= 0) & (places < whole)).astype(jnp.float32)


def window(array, shift_x, shift_y, shift_z, extent):
    return array[
        ...,
        3 + shift_x : 3 + shift_x + extent[0],
        3 + shift_y : 3 + shift_y + extent[1],
        3 + shift_z : 3 + shift_z + extent[2],
    ]


def pad_depth(array):
    return jnp.pad(array, [(0, 0)] * (array.ndim - 1) + [(3, 3)])


def on_device(rhs_force, integrity, contact, coarse_inverse):
    components, cells_x, cells_y, depth = rhs_force.shape
    bond_count = integrity.shape[0]
    aggregates = coarse_inverse.shape[0] // 3
    agg_depth = depth // aggregates
    agg_cells = cells_x * cells_y * agg_depth
    extent = (cells_x, cells_y, depth)
    offsets, unit_dirs, weights, nearest = bond_tables()
    slab_mask = rim_mask(cells_x, cells_x * lax.axis_size("slab"), lax.axis_index("slab"))
    col_mask = rim_mask(cells_y, cells_y * lax.axis_size("col"), lax.axis_index("col"))
    depth_mask = rim_mask(depth, depth, jnp.zeros((), jnp.int32))
    inside_pad = slab_mask[:, None, None] * col_mask[None, :, None] * depth_mask[None, None, :]

    def bond_shift(bond_index):
        return [int(entry) for entry in offsets[bond_index]]

    def heading_of(bond_index):
        return [float(unit_dirs[bond_index, component]) for component in range(3)]

    def rimmed(vector):
        return pad_depth(with_halo(vector, (("slab", 1), ("col", 2)), 3))

    lower_x = with_halo(integrity, (("slab", 1),), 3, high=False)
    spread = pad_depth(with_halo(lower_x, (("col", 2),), 3))
    contact_pad = pad_depth(
        with_halo(contact.astype(jnp.bfloat16), (("slab", 0), ("col", 1)), 3)
    ).astype(jnp.float32)
    near_contact = window(contact_pad, 0, 0, 0, extent)

    def bond_pair(bond_index):
        shift_x, shift_y, shift_z = bond_shift(bond_index)
        weight = float(weights[bond_index])
        level_pad = jnp.pad(spread[bond_index], ((0, 3), (0, 0), (0, 0)))
        intact = window(level_pad, 0, 0, 0, extent).astype(jnp.float32)
        prior = window(level_pad, -shift_x, -shift_y, -shift_z, extent).astype(jnp.float32)
        forward = weight * intact
        backward = weight * prior
        if nearest[bond_index] > 0.5:
            forward = forward + PENALTY * near_contact * window(
                contact_pad, shift_x, shift_y, shift_z, extent
            ) * (1.0 - intact)
            backward = backward + PENALTY * window(
                contact_pad, -shift_x, -shift_y, -shift_z, extent
            ) * near_contact * (1.0 - prior)
        forward = window(inside_pad, shift_x, shift_y, shift_z, extent) * forward
        return (forward, backward)

    diag_list = [jnp.full(extent, FOUNDATION, jnp.float32) for component in range(3)]
    for bond_index in range(bond_count):
        forward, backward = bond_pair(bond_index)
        heading = heading_of(bond_index)
        both_ends = forward + backward
        for component in range(3):
            diag_list[component] = (
                diag_list[component] + heading[component] * heading[component] * both_ends
            )
    diagonal = jnp.stack(diag_list)

    def operator(vector):
        padded = rimmed(vector)
        summed = [FOUNDATION * vector[component] for component in range(3)]
        for bond_index in range(bond_count):
            shift_x, shift_y, shift_z = bond_shift(bond_index)
            forward, backward = bond_pair(bond_index)
            heading = heading_of(bond_index)
            ahead_part = heading[0] * (
                vector[0] - window(padded[0], shift_x, shift_y, shift_z, extent)
            )
            behind_part = heading[0] * (
                vector[0] - window(padded[0], -shift_x, -shift_y, -shift_z, extent)
            )
            for component in range(1, 3):
                ahead_part = ahead_part + heading[component] * (
                    vector[component] - window(padded[component], shift_x, shift_y, shift_z, extent)
                )
                behind_part = behind_part + heading[component] * (
                    vector[component]
                    - window(padded[component], -shift_x, -shift_y, -shift_z, extent)
                )
            stretch = forward * ahead_part + backward * behind_part
            for component in range(3):
                summed[component] = summed[component] + heading[component] * stretch
        return jnp.stack(summed)

    def local_means(vector):
        blocks = vector.reshape(3, cells_x * cells_y, aggregates, agg_depth)
        return (jnp.sum(blocks, axis=(1, 3)) / agg_cells).T.reshape(3 * aggregates)

    def precondition(vector, coarse):
        solved = jnp.dot(coarse_inverse, coarse, precision=lax.Precision.HIGHEST)
        spread_back = solved.reshape(aggregates, 3).T[:, None, :, None]
        scaled = (vector / diagonal).reshape(
            3, cells_x * cells_y, aggregates, agg_depth
        ) + spread_back
        return scaled.reshape(vector.shape)

    every = ("slab", "col")

    residual = rhs_force
    coarse_now = device_rows(local_means(residual), every).reshape(-1)
    direction = precondition(residual, coarse_now)
    image_vec = operator(direction)
    sums = device_rows(
        jnp.concatenate(
            [
                jnp.stack([jnp.sum(residual * direction), jnp.sum(direction * image_vec)]),
                local_means(image_vec),
            ]
        ),
        every,
    )
    rz_now = jnp.sum(sums[:, 0])
    curvature = jnp.sum(sums[:, 1])
    step_size = rz_now / curvature
    image_means = sums[:, 2:].reshape(-1)
    displacement = step_size * direction
    residual = residual - step_size * image_vec
    for iteration in range(1, ITERS):
        more = iteration + 1 < ITERS
        coarse_now = coarse_now - step_size * image_means
        precond_r = precondition(residual, coarse_now)
        image_z = operator(precond_r)
        parts = [
            jnp.stack(
                [
                    jnp.sum(residual * precond_r),
                    jnp.sum(precond_r * image_z),
                    jnp.sum(precond_r * image_vec),
                    jnp.sum(direction * image_z),
                ]
            )
        ]
        if more:
            parts.append(local_means(image_z))
        sums = device_rows(jnp.concatenate(parts), every)
        fresh_rz = jnp.sum(sums[:, 0])
        ratio = fresh_rz / rz_now
        curvature = (
            jnp.sum(sums[:, 1])
            + ratio * (jnp.sum(sums[:, 2]) + jnp.sum(sums[:, 3]))
            + ratio * ratio * curvature
        )
        rz_now = fresh_rz
        direction = precond_r + ratio * direction
        image_vec = image_z + ratio * image_vec
        step_size = rz_now / curvature
        if more:
            image_means = sums[:, 4:].reshape(-1) + ratio * image_means
        displacement = displacement + step_size * direction
        residual = residual - step_size * image_vec
    return (displacement, residual)


def solution(mesh):
    return jax.shard_map(
        on_device,
        mesh=mesh,
        in_specs=(
            P(None, "slab", "col", None),
            P(None, "slab", "col", None),
            P("slab", "col", None),
            P(("slab", "col"), None),
        ),
        out_specs=(P(None, "slab", "col", None), P(None, "slab", "col", None)),
        check_vma=False,
    )
```

```python
import jax
import jax.numpy as jnp
import numpy as np
from jax import lax
from jax.sharding import PartitionSpec as P

ITERS = 2


STIFFNESS = 0.6
PENALTY = 2.0
FOUNDATION = 1.0


def with_halo(x, sides, width, low=True, high=True):
    for axis, dim in sides:
        count, length = (lax.axis_size(axis), x.shape[dim])
        up = [(i, (i + 1) % count) for i in range(count - 1)]
        down = [(j, i) for i, j in up]
        last = lax.slice_in_dim(x, length - width, length, axis=dim)
        first = lax.slice_in_dim(x, 0, width, axis=dim)
        parts = [x]
        if low:
            parts.insert(0, lax.ppermute(last, axis, up))
        if high:
            parts.append(lax.ppermute(first, axis, down))
        x = jnp.concatenate(parts, axis=dim)
    return x


def neighbourhood(x, x_dim, y_dim, width, blocks):
    slabs, cols = (lax.axis_size("slab"), lax.axis_size("col"))
    lengths = {x_dim: x.shape[x_dim], y_dim: x.shape[y_dim]}

    def side(array, dim, offset):
        if offset < 0:
            return lax.slice_in_dim(array, lengths[dim] - width, lengths[dim], axis=dim)
        if offset > 0:
            return lax.slice_in_dim(array, 0, width, axis=dim)
        return array

    grid = {(0, 0): x}
    for off_x, off_y in blocks:
        piece = side(side(x, x_dim, off_x), y_dim, off_y)
        pairs = [
            (s * cols + c, (s - off_x) * cols + (c - off_y))
            for s in range(slabs)
            for c in range(cols)
            if 0 <= s - off_x < slabs and 0 <= c - off_y < cols
        ]
        grid[(off_x, off_y)] = lax.ppermute(piece, ("slab", "col"), pairs)
    rows = []
    for off_x in (-1, 0, 1):
        cells = []
        for off_y in (-1, 0, 1):
            if (off_x, off_y) in grid:
                cells.append(grid[(off_x, off_y)])
            else:
                shape = list(x.shape)
                shape[x_dim] = width if off_x else lengths[x_dim]
                shape[y_dim] = width if off_y else lengths[y_dim]
                cells.append(jnp.zeros(shape, x.dtype))
        rows.append(jnp.concatenate(cells, axis=y_dim))
    return jnp.concatenate(rows, axis=x_dim)


def device_rows(vector, axes):
    count = 1
    for axis in axes:
        count = count * lax.axis_size(axis)
    tiled = jnp.broadcast_to(vector[None], (count,) + vector.shape)
    return lax.all_to_all(tiled, axes, 0, 0, tiled=True)


def bond_list():
    listed = []
    for shift_x in range(-3, 4):
        for shift_y in range(-3, 4):
            for shift_z in range(-3, 4):
                radius = shift_x * shift_x + shift_y * shift_y + shift_z * shift_z
                if 0 < radius <= 9 and (shift_x, shift_y, shift_z) > (0, 0, 0):
                    listed.append((shift_x, shift_y, shift_z))
    return listed


def bond_tables():
    offsets = np.array(bond_list(), dtype=np.int32)
    lengths = np.sqrt(np.sum(offsets * offsets, axis=1).astype(np.float32)).astype(np.float32)
    unit_dirs = (offsets.astype(np.float32) / lengths[:, None]).astype(np.float32)
    weights = (np.float32(STIFFNESS) / lengths).astype(np.float32)
    nearest = (lengths < 1.5).astype(np.float32)
    return (offsets, unit_dirs, weights, nearest)


def rim_mask(count, whole, position):
    places = position * count + jnp.arange(count + 6, dtype=jnp.int32) - 3
    return ((places >= 0) & (places < whole)).astype(jnp.float32)


def window(array, shift_x, shift_y, shift_z, extent):
    return array[
        ...,
        3 + shift_x : 3 + shift_x + extent[0],
        3 + shift_y : 3 + shift_y + extent[1],
        3 + shift_z : 3 + shift_z + extent[2],
    ]


def pad_depth(array):
    return jnp.pad(array, [(0, 0)] * (array.ndim - 1) + [(3, 3)])


def on_device(rhs_force, integrity, contact, coarse_inverse):
    components, cells_x, cells_y, depth = rhs_force.shape
    bond_count = integrity.shape[0]
    aggregates = coarse_inverse.shape[0] // 3
    agg_depth = depth // aggregates
    agg_cells = cells_x * cells_y * agg_depth
    extent = (cells_x, cells_y, depth)
    offsets, unit_dirs, weights, nearest = bond_tables()
    slab_mask = rim_mask(cells_x, cells_x * lax.axis_size("slab"), lax.axis_index("slab"))
    col_mask = rim_mask(cells_y, cells_y * lax.axis_size("col"), lax.axis_index("col"))
    depth_mask = rim_mask(depth, depth, jnp.zeros((), jnp.int32))
    inside_pad = slab_mask[:, None, None] * col_mask[None, :, None] * depth_mask[None, None, :]

    def bond_shift(bond_index):
        return [int(entry) for entry in offsets[bond_index]]

    def heading_of(bond_index):
        return [float(unit_dirs[bond_index, component]) for component in range(3)]

    every_side = [(a, b) for a in (-1, 0, 1) for b in (-1, 0, 1) if (a, b) != (0, 0)]
    lower_sides = [(-1, -1), (-1, 0), (-1, 1), (0, -1), (0, 1)]

    def rimmed(vector):
        return pad_depth(neighbourhood(vector, 1, 2, 3, every_side))

    contact_flags = contact.astype(jnp.bfloat16)
    stacked = jnp.concatenate([integrity, contact_flags[None]], axis=0)
    spread = pad_depth(neighbourhood(stacked, 1, 2, 3, lower_sides))
    upper_contact = neighbourhood(contact_flags, 0, 1, 3, [(1, -1), (1, 0), (1, 1)])
    contact_pad = jnp.concatenate(
        [spread[bond_count][: cells_x + 3], pad_depth(upper_contact[cells_x + 3 :])], axis=0
    ).astype(jnp.float32)
    near_contact = window(contact_pad, 0, 0, 0, extent)

    def bond_pair(bond_index):
        shift_x, shift_y, shift_z = bond_shift(bond_index)
        weight = float(weights[bond_index])
        level_pad = spread[bond_index]
        intact = window(level_pad, 0, 0, 0, extent).astype(jnp.float32)
        prior = window(level_pad, -shift_x, -shift_y, -shift_z, extent).astype(jnp.float32)
        forward = weight * intact
        backward = weight * prior
        if nearest[bond_index] > 0.5:
            forward = forward + PENALTY * near_contact * window(
                contact_pad, shift_x, shift_y, shift_z, extent
            ) * (1.0 - intact)
            backward = backward + PENALTY * window(
                contact_pad, -shift_x, -shift_y, -shift_z, extent
            ) * near_contact * (1.0 - prior)
        forward = window(inside_pad, shift_x, shift_y, shift_z, extent) * forward
        return (forward, backward)

    diag_list = [jnp.full(extent, FOUNDATION, jnp.float32) for component in range(3)]
    for bond_index in range(bond_count):
        forward, backward = bond_pair(bond_index)
        heading = heading_of(bond_index)
        both_ends = forward + backward
        for component in range(3):
            diag_list[component] = (
                diag_list[component] + heading[component] * heading[component] * both_ends
            )
    diagonal = jnp.stack(diag_list)

    def operator(vector):
        padded = rimmed(vector)
        summed = [FOUNDATION * vector[component] for component in range(3)]
        for bond_index in range(bond_count):
            shift_x, shift_y, shift_z = bond_shift(bond_index)
            forward, backward = bond_pair(bond_index)
            heading = heading_of(bond_index)
            ahead_part = heading[0] * (
                vector[0] - window(padded[0], shift_x, shift_y, shift_z, extent)
            )
            behind_part = heading[0] * (
                vector[0] - window(padded[0], -shift_x, -shift_y, -shift_z, extent)
            )
            for component in range(1, 3):
                ahead_part = ahead_part + heading[component] * (
                    vector[component] - window(padded[component], shift_x, shift_y, shift_z, extent)
                )
                behind_part = behind_part + heading[component] * (
                    vector[component]
                    - window(padded[component], -shift_x, -shift_y, -shift_z, extent)
                )
            stretch = forward * ahead_part + backward * behind_part
            for component in range(3):
                summed[component] = summed[component] + heading[component] * stretch
        return jnp.stack(summed)

    def local_means(vector):
        blocks = vector.reshape(3, cells_x * cells_y, aggregates, agg_depth)
        return (jnp.sum(blocks, axis=(1, 3)) / agg_cells).T.reshape(3 * aggregates)

    def precondition(vector, coarse):
        solved = jnp.dot(coarse_inverse, coarse, precision=lax.Precision.HIGHEST)
        spread_back = solved.reshape(aggregates, 3).T[:, None, :, None]
        scaled = (vector / diagonal).reshape(
            3, cells_x * cells_y, aggregates, agg_depth
        ) + spread_back
        return scaled.reshape(vector.shape)

    every = ("slab", "col")

    residual = rhs_force
    coarse_now = device_rows(local_means(residual), every).reshape(-1)
    direction = precondition(residual, coarse_now)
    image_vec = operator(direction)
    sums = device_rows(
        jnp.concatenate(
            [
                jnp.stack([jnp.sum(residual * direction), jnp.sum(direction * image_vec)]),
                local_means(image_vec),
            ]
        ),
        every,
    )
    rz_now = jnp.sum(sums[:, 0])
    curvature = jnp.sum(sums[:, 1])
    step_size = rz_now / curvature
    image_means = sums[:, 2:].reshape(-1)
    displacement = step_size * direction
    residual = residual - step_size * image_vec
    for iteration in range(1, ITERS):
        more = iteration + 1 < ITERS
        coarse_now = coarse_now - step_size * image_means
        precond_r = precondition(residual, coarse_now)
        image_z = operator(precond_r)
        parts = [
            jnp.stack(
                [
                    jnp.sum(residual * precond_r),
                    jnp.sum(precond_r * image_z),
                    jnp.sum(precond_r * image_vec),
                    jnp.sum(direction * image_z),
                ]
            )
        ]
        if more:
            parts.append(local_means(image_z))
        sums = device_rows(jnp.concatenate(parts), every)
        fresh_rz = jnp.sum(sums[:, 0])
        ratio = fresh_rz / rz_now
        curvature = (
            jnp.sum(sums[:, 1])
            + ratio * (jnp.sum(sums[:, 2]) + jnp.sum(sums[:, 3]))
            + ratio * ratio * curvature
        )
        rz_now = fresh_rz
        direction = precond_r + ratio * direction
        image_vec = image_z + ratio * image_vec
        step_size = rz_now / curvature
        if more:
            image_means = sums[:, 4:].reshape(-1) + ratio * image_means
        displacement = displacement + step_size * direction
        residual = residual - step_size * image_vec
    return (displacement, residual)


def solution(mesh):
    return jax.shard_map(
        on_device,
        mesh=mesh,
        in_specs=(
            P(None, "slab", "col", None),
            P(None, "slab", "col", None),
            P("slab", "col", None),
            P(("slab", "col"), None),
        ),
        out_specs=(P(None, "slab", "col", None), P(None, "slab", "col", None)),
        check_vma=False,
    )
```

```python
import jax
import jax.numpy as jnp
import numpy as np
from jax import lax
from jax.sharding import PartitionSpec as P

ITERS = 2


STIFFNESS = 0.6
PENALTY = 2.0
FOUNDATION = 1.0


def with_halo(x, sides, width, low=True, high=True):
    for axis, dim in sides:
        count, length = (lax.axis_size(axis), x.shape[dim])
        up = [(i, (i + 1) % count) for i in range(count - 1)]
        down = [(j, i) for i, j in up]
        last = lax.slice_in_dim(x, length - width, length, axis=dim)
        first = lax.slice_in_dim(x, 0, width, axis=dim)
        parts = [x]
        if low:
            parts.insert(0, lax.ppermute(last, axis, up))
        if high:
            parts.append(lax.ppermute(first, axis, down))
        x = jnp.concatenate(parts, axis=dim)
    return x


def device_rows(vector, axes):
    count = 1
    for axis in axes:
        count = count * lax.axis_size(axis)
    tiled = jnp.broadcast_to(vector[None], (count,) + vector.shape)
    return lax.all_to_all(tiled, axes, 0, 0, tiled=True)


def bond_list():
    listed = []
    for shift_x in range(-3, 4):
        for shift_y in range(-3, 4):
            for shift_z in range(-3, 4):
                radius = shift_x * shift_x + shift_y * shift_y + shift_z * shift_z
                if 0 < radius <= 9 and (shift_x, shift_y, shift_z) > (0, 0, 0):
                    listed.append((shift_x, shift_y, shift_z))
    return listed


def bond_tables():
    offsets = np.array(bond_list(), dtype=np.int32)
    lengths = np.sqrt(np.sum(offsets * offsets, axis=1).astype(np.float32)).astype(np.float32)
    unit_dirs = (offsets.astype(np.float32) / lengths[:, None]).astype(np.float32)
    weights = (np.float32(STIFFNESS) / lengths).astype(np.float32)
    nearest = (lengths < 1.5).astype(np.float32)
    return (offsets, unit_dirs, weights, nearest)


def rim_mask(count, whole, position):
    places = position * count + jnp.arange(count + 6, dtype=jnp.int32) - 3
    return ((places >= 0) & (places < whole)).astype(jnp.float32)


def window(array, shift_x, shift_y, shift_z, extent):
    return array[
        ...,
        3 + shift_x : 3 + shift_x + extent[0],
        3 + shift_y : 3 + shift_y + extent[1],
        3 + shift_z : 3 + shift_z + extent[2],
    ]


def pad_depth(array):
    return jnp.pad(array, [(0, 0)] * (array.ndim - 1) + [(3, 3)])


def on_device(rhs_force, integrity, contact, coarse_inverse):
    components, cells_x, cells_y, depth = rhs_force.shape
    bond_count = integrity.shape[0]
    aggregates = coarse_inverse.shape[0] // 3
    agg_depth = depth // aggregates
    agg_cells = cells_x * cells_y * agg_depth
    extent = (cells_x, cells_y, depth)
    offsets, unit_dirs, weights, nearest = bond_tables()
    slab_mask = rim_mask(cells_x, cells_x * lax.axis_size("slab"), lax.axis_index("slab"))
    col_mask = rim_mask(cells_y, cells_y * lax.axis_size("col"), lax.axis_index("col"))
    depth_mask = rim_mask(depth, depth, jnp.zeros((), jnp.int32))
    inside_pad = slab_mask[:, None, None] * col_mask[None, :, None] * depth_mask[None, None, :]

    def bond_shift(bond_index):
        return [int(entry) for entry in offsets[bond_index]]

    def heading_of(bond_index):
        return [float(unit_dirs[bond_index, component]) for component in range(3)]

    def rimmed(vector):
        return pad_depth(with_halo(vector, (("slab", 1), ("col", 2)), 3))

    contact_flags = contact.astype(jnp.bfloat16)
    stacked = jnp.concatenate([integrity, contact_flags[None]], axis=0)
    lower_x = with_halo(stacked, (("slab", 1),), 3, high=False)
    upper_x = with_halo(contact_flags, (("slab", 0),), 3, low=False)[cells_x:]
    lower_x = jnp.concatenate(
        [
            lower_x,
            jnp.concatenate(
                [jnp.zeros((bond_count,) + upper_x.shape, upper_x.dtype), upper_x[None]], axis=0
            ),
        ],
        axis=1,
    )
    spread = pad_depth(with_halo(lower_x, (("col", 2),), 3))
    contact_pad = spread[bond_count].astype(jnp.float32)
    near_contact = window(contact_pad, 0, 0, 0, extent)

    def bond_pair(bond_index):
        shift_x, shift_y, shift_z = bond_shift(bond_index)
        weight = float(weights[bond_index])
        level_pad = spread[bond_index]
        intact = window(level_pad, 0, 0, 0, extent).astype(jnp.float32)
        prior = window(level_pad, -shift_x, -shift_y, -shift_z, extent).astype(jnp.float32)
        forward = weight * intact
        backward = weight * prior
        if nearest[bond_index] > 0.5:
            forward = forward + PENALTY * near_contact * window(
                contact_pad, shift_x, shift_y, shift_z, extent
            ) * (1.0 - intact)
            backward = backward + PENALTY * window(
                contact_pad, -shift_x, -shift_y, -shift_z, extent
            ) * near_contact * (1.0 - prior)
        forward = window(inside_pad, shift_x, shift_y, shift_z, extent) * forward
        return (forward, backward)

    diag_list = [jnp.full(extent, FOUNDATION, jnp.float32) for component in range(3)]
    for bond_index in range(bond_count):
        forward, backward = bond_pair(bond_index)
        heading = heading_of(bond_index)
        both_ends = forward + backward
        for component in range(3):
            diag_list[component] = (
                diag_list[component] + heading[component] * heading[component] * both_ends
            )
    diagonal = jnp.stack(diag_list)

    def operator(vector):
        padded = rimmed(vector)
        summed = [FOUNDATION * vector[component] for component in range(3)]
        for bond_index in range(bond_count):
            shift_x, shift_y, shift_z = bond_shift(bond_index)
            forward, backward = bond_pair(bond_index)
            heading = heading_of(bond_index)
            ahead_part = heading[0] * (
                vector[0] - window(padded[0], shift_x, shift_y, shift_z, extent)
            )
            behind_part = heading[0] * (
                vector[0] - window(padded[0], -shift_x, -shift_y, -shift_z, extent)
            )
            for component in range(1, 3):
                ahead_part = ahead_part + heading[component] * (
                    vector[component] - window(padded[component], shift_x, shift_y, shift_z, extent)
                )
                behind_part = behind_part + heading[component] * (
                    vector[component]
                    - window(padded[component], -shift_x, -shift_y, -shift_z, extent)
                )
            stretch = forward * ahead_part + backward * behind_part
            for component in range(3):
                summed[component] = summed[component] + heading[component] * stretch
        return jnp.stack(summed)

    def local_means(vector):
        blocks = vector.reshape(3, cells_x * cells_y, aggregates, agg_depth)
        return (jnp.sum(blocks, axis=(1, 3)) / agg_cells).T.reshape(3 * aggregates)

    def precondition(vector, coarse):
        solved = jnp.dot(coarse_inverse, coarse, precision=lax.Precision.HIGHEST)
        spread_back = solved.reshape(aggregates, 3).T[:, None, :, None]
        scaled = (vector / diagonal).reshape(
            3, cells_x * cells_y, aggregates, agg_depth
        ) + spread_back
        return scaled.reshape(vector.shape)

    every = ("slab", "col")

    residual = rhs_force
    coarse_now = device_rows(local_means(residual), every).reshape(-1)
    direction = precondition(residual, coarse_now)
    image_vec = operator(direction)
    sums = device_rows(
        jnp.concatenate(
            [
                jnp.stack([jnp.sum(residual * direction), jnp.sum(direction * image_vec)]),
                local_means(image_vec),
            ]
        ),
        every,
    )
    rz_now = jnp.sum(sums[:, 0])
    curvature = jnp.sum(sums[:, 1])
    step_size = rz_now / curvature
    image_means = sums[:, 2:].reshape(-1)
    displacement = step_size * direction
    residual = residual - step_size * image_vec
    for iteration in range(1, ITERS):
        more = iteration + 1 < ITERS
        coarse_now = coarse_now - step_size * image_means
        precond_r = precondition(residual, coarse_now)
        image_z = operator(precond_r)
        parts = [
            jnp.stack(
                [
                    jnp.sum(residual * precond_r),
                    jnp.sum(precond_r * image_z),
                    jnp.sum(precond_r * image_vec),
                    jnp.sum(direction * image_z),
                ]
            )
        ]
        if more:
            parts.append(local_means(image_z))
        sums = device_rows(jnp.concatenate(parts), every)
        fresh_rz = jnp.sum(sums[:, 0])
        ratio = fresh_rz / rz_now
        curvature = (
            jnp.sum(sums[:, 1])
            + ratio * (jnp.sum(sums[:, 2]) + jnp.sum(sums[:, 3]))
            + ratio * ratio * curvature
        )
        rz_now = fresh_rz
        direction = precond_r + ratio * direction
        image_vec = image_z + ratio * image_vec
        step_size = rz_now / curvature
        if more:
            image_means = sums[:, 4:].reshape(-1) + ratio * image_means
        displacement = displacement + step_size * direction
        residual = residual - step_size * image_vec
    return (displacement, residual)


def solution(mesh):
    return jax.shard_map(
        on_device,
        mesh=mesh,
        in_specs=(
            P(None, "slab", "col", None),
            P(None, "slab", "col", None),
            P("slab", "col", None),
            P(("slab", "col"), None),
        ),
        out_specs=(P(None, "slab", "col", None), P(None, "slab", "col", None)),
        check_vma=False,
    )
```

```python
import jax
import jax.numpy as jnp
import numpy as np
from jax import lax
from jax.sharding import PartitionSpec as P

ITERS = 2


STIFFNESS = 0.6
PENALTY = 2.0
FOUNDATION = 1.0


def with_halo(x, sides, width, low=True, high=True):
    for axis, dim in sides:
        count, length = (lax.axis_size(axis), x.shape[dim])
        up = [(i, (i + 1) % count) for i in range(count - 1)]
        down = [(j, i) for i, j in up]
        last = lax.slice_in_dim(x, length - width, length, axis=dim)
        first = lax.slice_in_dim(x, 0, width, axis=dim)
        parts = [x]
        if low:
            parts.insert(0, lax.ppermute(last, axis, up))
        if high:
            parts.append(lax.ppermute(first, axis, down))
        x = jnp.concatenate(parts, axis=dim)
    return x


def lower_rows(levels, reach, width):
    count, length = (lax.axis_size("slab"), levels.shape[1])
    up = [(i, i + 1) for i in range(count - 1)]
    starts = [int(np.argmax(reach >= depth)) for depth in range(1, width + 1)]
    sent = jnp.concatenate(
        [levels[start:, length - depth] for depth, start in zip(range(1, width + 1), starts)], axis=0
    )
    got = lax.ppermute(sent, "slab", up)
    rows, at = ({}, 0)
    for depth, start in zip(range(1, width + 1), starts):
        size = levels.shape[0] - start
        rows[depth] = jnp.concatenate(
            [jnp.zeros((start,) + levels.shape[2:], levels.dtype), got[at : at + size]], axis=0
        )
        at = at + size
    return jnp.stack([rows[depth] for depth in range(width, 0, -1)], axis=1)


def device_rows(vector, axes):
    count = 1
    for axis in axes:
        count = count * lax.axis_size(axis)
    tiled = jnp.broadcast_to(vector[None], (count,) + vector.shape)
    return lax.all_to_all(tiled, axes, 0, 0, tiled=True)


def bond_list():
    listed = []
    for shift_x in range(-3, 4):
        for shift_y in range(-3, 4):
            for shift_z in range(-3, 4):
                radius = shift_x * shift_x + shift_y * shift_y + shift_z * shift_z
                if 0 < radius <= 9 and (shift_x, shift_y, shift_z) > (0, 0, 0):
                    listed.append((shift_x, shift_y, shift_z))
    return listed


def bond_tables():
    offsets = np.array(bond_list(), dtype=np.int32)
    lengths = np.sqrt(np.sum(offsets * offsets, axis=1).astype(np.float32)).astype(np.float32)
    unit_dirs = (offsets.astype(np.float32) / lengths[:, None]).astype(np.float32)
    weights = (np.float32(STIFFNESS) / lengths).astype(np.float32)
    nearest = (lengths < 1.5).astype(np.float32)
    return (offsets, unit_dirs, weights, nearest)


def rim_mask(count, whole, position):
    places = position * count + jnp.arange(count + 6, dtype=jnp.int32) - 3
    return ((places >= 0) & (places < whole)).astype(jnp.float32)


def window(array, shift_x, shift_y, shift_z, extent):
    return array[
        ...,
        3 + shift_x : 3 + shift_x + extent[0],
        3 + shift_y : 3 + shift_y + extent[1],
        3 + shift_z : 3 + shift_z + extent[2],
    ]


def pad_depth(array):
    return jnp.pad(array, [(0, 0)] * (array.ndim - 1) + [(3, 3)])


def on_device(rhs_force, integrity, contact, coarse_inverse):
    components, cells_x, cells_y, depth = rhs_force.shape
    bond_count = integrity.shape[0]
    aggregates = coarse_inverse.shape[0] // 3
    agg_depth = depth // aggregates
    agg_cells = cells_x * cells_y * agg_depth
    extent = (cells_x, cells_y, depth)
    offsets, unit_dirs, weights, nearest = bond_tables()
    slab_mask = rim_mask(cells_x, cells_x * lax.axis_size("slab"), lax.axis_index("slab"))
    col_mask = rim_mask(cells_y, cells_y * lax.axis_size("col"), lax.axis_index("col"))
    depth_mask = rim_mask(depth, depth, jnp.zeros((), jnp.int32))
    inside_pad = slab_mask[:, None, None] * col_mask[None, :, None] * depth_mask[None, None, :]

    def bond_shift(bond_index):
        return [int(entry) for entry in offsets[bond_index]]

    def heading_of(bond_index):
        return [float(unit_dirs[bond_index, component]) for component in range(3)]

    def rimmed(vector):
        return pad_depth(with_halo(vector, (("slab", 1), ("col", 2)), 3))

    lower_x = jnp.concatenate([lower_rows(integrity, offsets[:, 0], 3), integrity], axis=1)
    spread = pad_depth(with_halo(lower_x, (("col", 2),), 3))
    contact_pad = pad_depth(
        with_halo(contact.astype(jnp.bfloat16), (("slab", 0), ("col", 1)), 3)
    ).astype(jnp.float32)
    near_contact = window(contact_pad, 0, 0, 0, extent)

    def bond_pair(bond_index):
        shift_x, shift_y, shift_z = bond_shift(bond_index)
        weight = float(weights[bond_index])
        level_pad = jnp.pad(spread[bond_index], ((0, 3), (0, 0), (0, 0)))
        intact = window(level_pad, 0, 0, 0, extent).astype(jnp.float32)
        prior = window(level_pad, -shift_x, -shift_y, -shift_z, extent).astype(jnp.float32)
        forward = weight * intact
        backward = weight * prior
        if nearest[bond_index] > 0.5:
            forward = forward + PENALTY * near_contact * window(
                contact_pad, shift_x, shift_y, shift_z, extent
            ) * (1.0 - intact)
            backward = backward + PENALTY * window(
                contact_pad, -shift_x, -shift_y, -shift_z, extent
            ) * near_contact * (1.0 - prior)
        forward = window(inside_pad, shift_x, shift_y, shift_z, extent) * forward
        return (forward, backward)

    diag_list = [jnp.full(extent, FOUNDATION, jnp.float32) for component in range(3)]
    for bond_index in range(bond_count):
        forward, backward = bond_pair(bond_index)
        heading = heading_of(bond_index)
        both_ends = forward + backward
        for component in range(3):
            diag_list[component] = (
                diag_list[component] + heading[component] * heading[component] * both_ends
            )
    diagonal = jnp.stack(diag_list)

    def operator(vector):
        padded = rimmed(vector)
        summed = [FOUNDATION * vector[component] for component in range(3)]
        for bond_index in range(bond_count):
            shift_x, shift_y, shift_z = bond_shift(bond_index)
            forward, backward = bond_pair(bond_index)
            heading = heading_of(bond_index)
            ahead_part = heading[0] * (
                vector[0] - window(padded[0], shift_x, shift_y, shift_z, extent)
            )
            behind_part = heading[0] * (
                vector[0] - window(padded[0], -shift_x, -shift_y, -shift_z, extent)
            )
            for component in range(1, 3):
                ahead_part = ahead_part + heading[component] * (
                    vector[component] - window(padded[component], shift_x, shift_y, shift_z, extent)
                )
                behind_part = behind_part + heading[component] * (
                    vector[component]
                    - window(padded[component], -shift_x, -shift_y, -shift_z, extent)
                )
            stretch = forward * ahead_part + backward * behind_part
            for component in range(3):
                summed[component] = summed[component] + heading[component] * stretch
        return jnp.stack(summed)

    def local_means(vector):
        blocks = vector.reshape(3, cells_x * cells_y, aggregates, agg_depth)
        return (jnp.sum(blocks, axis=(1, 3)) / agg_cells).T.reshape(3 * aggregates)

    def precondition(vector, coarse):
        solved = jnp.dot(coarse_inverse, coarse, precision=lax.Precision.HIGHEST)
        spread_back = solved.reshape(aggregates, 3).T[:, None, :, None]
        scaled = (vector / diagonal).reshape(
            3, cells_x * cells_y, aggregates, agg_depth
        ) + spread_back
        return scaled.reshape(vector.shape)

    every = ("slab", "col")

    residual = rhs_force
    coarse_now = device_rows(local_means(residual), every).reshape(-1)
    direction = precondition(residual, coarse_now)
    image_vec = operator(direction)
    sums = device_rows(
        jnp.concatenate(
            [
                jnp.stack([jnp.sum(residual * direction), jnp.sum(direction * image_vec)]),
                local_means(image_vec),
            ]
        ),
        every,
    )
    rz_now = jnp.sum(sums[:, 0])
    curvature = jnp.sum(sums[:, 1])
    step_size = rz_now / curvature
    image_means = sums[:, 2:].reshape(-1)
    displacement = step_size * direction
    residual = residual - step_size * image_vec
    for iteration in range(1, ITERS):
        more = iteration + 1 < ITERS
        coarse_now = coarse_now - step_size * image_means
        precond_r = precondition(residual, coarse_now)
        image_z = operator(precond_r)
        parts = [
            jnp.stack(
                [
                    jnp.sum(residual * precond_r),
                    jnp.sum(precond_r * image_z),
                    jnp.sum(precond_r * image_vec),
                    jnp.sum(direction * image_z),
                ]
            )
        ]
        if more:
            parts.append(local_means(image_z))
        sums = device_rows(jnp.concatenate(parts), every)
        fresh_rz = jnp.sum(sums[:, 0])
        ratio = fresh_rz / rz_now
        curvature = (
            jnp.sum(sums[:, 1])
            + ratio * (jnp.sum(sums[:, 2]) + jnp.sum(sums[:, 3]))
            + ratio * ratio * curvature
        )
        rz_now = fresh_rz
        direction = precond_r + ratio * direction
        image_vec = image_z + ratio * image_vec
        step_size = rz_now / curvature
        if more:
            image_means = sums[:, 4:].reshape(-1) + ratio * image_means
        displacement = displacement + step_size * direction
        residual = residual - step_size * image_vec
    return (displacement, residual)


def solution(mesh):
    return jax.shard_map(
        on_device,
        mesh=mesh,
        in_specs=(
            P(None, "slab", "col", None),
            P(None, "slab", "col", None),
            P("slab", "col", None),
            P(("slab", "col"), None),
        ),
        out_specs=(P(None, "slab", "col", None), P(None, "slab", "col", None)),
        check_vma=False,
    )
```

```python
import jax
import jax.numpy as jnp
import numpy as np
from jax import lax
from jax.sharding import PartitionSpec as P

ITERS = 2


STIFFNESS = 0.6
PENALTY = 2.0
FOUNDATION = 1.0


def with_halo(x, sides, width, low=True, high=True):
    for axis, dim in sides:
        count, length = (lax.axis_size(axis), x.shape[dim])
        up = [(i, (i + 1) % count) for i in range(count - 1)]
        down = [(j, i) for i, j in up]
        last = lax.slice_in_dim(x, length - width, length, axis=dim)
        first = lax.slice_in_dim(x, 0, width, axis=dim)
        parts = [x]
        if low:
            parts.insert(0, lax.ppermute(last, axis, up))
        if high:
            parts.append(lax.ppermute(first, axis, down))
        x = jnp.concatenate(parts, axis=dim)
    return x


def lower_rows(levels, reach, width):
    count, length = (lax.axis_size("slab"), levels.shape[1])
    up = [(i, i + 1) for i in range(count - 1)]
    starts = [int(np.argmax(reach >= depth)) for depth in range(1, width + 1)]
    sent = jnp.concatenate(
        [levels[start:, length - depth] for depth, start in zip(range(1, width + 1), starts)], axis=0
    )
    got = lax.ppermute(sent, "slab", up)
    rows, at = ({}, 0)
    for depth, start in zip(range(1, width + 1), starts):
        size = levels.shape[0] - start
        rows[depth] = jnp.concatenate(
            [jnp.zeros((start,) + levels.shape[2:], levels.dtype), got[at : at + size]], axis=0
        )
        at = at + size
    return jnp.stack([rows[depth] for depth in range(width, 0, -1)], axis=1)


def device_rows(vector, axes):
    count = 1
    for axis in axes:
        count = count * lax.axis_size(axis)
    tiled = jnp.broadcast_to(vector[None], (count,) + vector.shape)
    return lax.all_to_all(tiled, axes, 0, 0, tiled=True)


def bond_list():
    listed = []
    for shift_x in range(-3, 4):
        for shift_y in range(-3, 4):
            for shift_z in range(-3, 4):
                radius = shift_x * shift_x + shift_y * shift_y + shift_z * shift_z
                if 0 < radius <= 9 and (shift_x, shift_y, shift_z) > (0, 0, 0):
                    listed.append((shift_x, shift_y, shift_z))
    return listed


def bond_tables():
    offsets = np.array(bond_list(), dtype=np.int32)
    lengths = np.sqrt(np.sum(offsets * offsets, axis=1).astype(np.float32)).astype(np.float32)
    unit_dirs = (offsets.astype(np.float32) / lengths[:, None]).astype(np.float32)
    weights = (np.float32(STIFFNESS) / lengths).astype(np.float32)
    nearest = (lengths < 1.5).astype(np.float32)
    return (offsets, unit_dirs, weights, nearest)


def rim_mask(count, whole, position):
    places = position * count + jnp.arange(count + 6, dtype=jnp.int32) - 3
    return ((places >= 0) & (places < whole)).astype(jnp.float32)


def window(array, shift_x, shift_y, shift_z, extent):
    return array[
        ...,
        3 + shift_x : 3 + shift_x + extent[0],
        3 + shift_y : 3 + shift_y + extent[1],
        3 + shift_z : 3 + shift_z + extent[2],
    ]


def pad_depth(array):
    return jnp.pad(array, [(0, 0)] * (array.ndim - 1) + [(3, 3)])


def on_device(rhs_force, integrity, contact, coarse_inverse):
    components, cells_x, cells_y, depth = rhs_force.shape
    bond_count = integrity.shape[0]
    aggregates = coarse_inverse.shape[0] // 3
    agg_depth = depth // aggregates
    agg_cells = cells_x * cells_y * agg_depth
    extent = (cells_x, cells_y, depth)
    offsets, unit_dirs, weights, nearest = bond_tables()
    slab_mask = rim_mask(cells_x, cells_x * lax.axis_size("slab"), lax.axis_index("slab"))
    col_mask = rim_mask(cells_y, cells_y * lax.axis_size("col"), lax.axis_index("col"))
    depth_mask = rim_mask(depth, depth, jnp.zeros((), jnp.int32))
    inside_pad = slab_mask[:, None, None] * col_mask[None, :, None] * depth_mask[None, None, :]

    def bond_shift(bond_index):
        return [int(entry) for entry in offsets[bond_index]]

    def heading_of(bond_index):
        return [float(unit_dirs[bond_index, component]) for component in range(3)]

    def rimmed(vector):
        return pad_depth(with_halo(vector, (("slab", 1), ("col", 2)), 3))

    lower_x = jnp.concatenate([lower_rows(integrity, offsets[:, 0], 3), integrity], axis=1)
    spread = pad_depth(with_halo(lower_x, (("col", 2),), 3))
    contact_pad = pad_depth(
        with_halo(contact.astype(jnp.bfloat16), (("slab", 0), ("col", 1)), 3)
    ).astype(jnp.float32)
    near_contact = window(contact_pad, 0, 0, 0, extent)

    def bond_pair(bond_index):
        shift_x, shift_y, shift_z = bond_shift(bond_index)
        weight = float(weights[bond_index])
        level_pad = jnp.pad(spread[bond_index], ((0, 3), (0, 0), (0, 0)))
        intact = window(level_pad, 0, 0, 0, extent).astype(jnp.float32)
        prior = window(level_pad, -shift_x, -shift_y, -shift_z, extent).astype(jnp.float32)
        forward = weight * intact
        backward = weight * prior
        if nearest[bond_index] > 0.5:
            forward = forward + PENALTY * near_contact * window(
                contact_pad, shift_x, shift_y, shift_z, extent
            ) * (1.0 - intact)
            backward = backward + PENALTY * window(
                contact_pad, -shift_x, -shift_y, -shift_z, extent
            ) * near_contact * (1.0 - prior)
        forward = window(inside_pad, shift_x, shift_y, shift_z, extent) * forward
        return (forward, backward)

    coefficients = lax.optimization_barrier(
        jnp.stack([jnp.stack(bond_pair(bond_index)) for bond_index in range(bond_count)])
    )
    diag_list = [jnp.full(extent, FOUNDATION, jnp.float32) for component in range(3)]
    for bond_index in range(bond_count):
        forward, backward = (coefficients[bond_index, 0], coefficients[bond_index, 1])
        heading = heading_of(bond_index)
        both_ends = forward + backward
        for component in range(3):
            diag_list[component] = (
                diag_list[component] + heading[component] * heading[component] * both_ends
            )
    diagonal = jnp.stack(diag_list)

    def operator(vector):
        padded = rimmed(vector)
        summed = [FOUNDATION * vector[component] for component in range(3)]
        for bond_index in range(bond_count):
            shift_x, shift_y, shift_z = bond_shift(bond_index)
            forward, backward = (coefficients[bond_index, 0], coefficients[bond_index, 1])
            heading = heading_of(bond_index)
            ahead_part = heading[0] * (
                vector[0] - window(padded[0], shift_x, shift_y, shift_z, extent)
            )
            behind_part = heading[0] * (
                vector[0] - window(padded[0], -shift_x, -shift_y, -shift_z, extent)
            )
            for component in range(1, 3):
                ahead_part = ahead_part + heading[component] * (
                    vector[component] - window(padded[component], shift_x, shift_y, shift_z, extent)
                )
                behind_part = behind_part + heading[component] * (
                    vector[component]
                    - window(padded[component], -shift_x, -shift_y, -shift_z, extent)
                )
            stretch = forward * ahead_part + backward * behind_part
            for component in range(3):
                summed[component] = summed[component] + heading[component] * stretch
        return jnp.stack(summed)

    def local_means(vector):
        blocks = vector.reshape(3, cells_x * cells_y, aggregates, agg_depth)
        return (jnp.sum(blocks, axis=(1, 3)) / agg_cells).T.reshape(3 * aggregates)

    def precondition(vector, coarse):
        solved = jnp.dot(coarse_inverse, coarse, precision=lax.Precision.HIGHEST)
        spread_back = solved.reshape(aggregates, 3).T[:, None, :, None]
        scaled = (vector / diagonal).reshape(
            3, cells_x * cells_y, aggregates, agg_depth
        ) + spread_back
        return scaled.reshape(vector.shape)

    every = ("slab", "col")

    residual = rhs_force
    coarse_now = device_rows(local_means(residual), every).reshape(-1)
    direction = precondition(residual, coarse_now)
    image_vec = operator(direction)
    sums = device_rows(
        jnp.concatenate(
            [
                jnp.stack([jnp.sum(residual * direction), jnp.sum(direction * image_vec)]),
                local_means(image_vec),
            ]
        ),
        every,
    )
    rz_now = jnp.sum(sums[:, 0])
    curvature = jnp.sum(sums[:, 1])
    step_size = rz_now / curvature
    image_means = sums[:, 2:].reshape(-1)
    displacement = step_size * direction
    residual = residual - step_size * image_vec
    for iteration in range(1, ITERS):
        more = iteration + 1 < ITERS
        coarse_now = coarse_now - step_size * image_means
        precond_r = precondition(residual, coarse_now)
        image_z = operator(precond_r)
        parts = [
            jnp.stack(
                [
                    jnp.sum(residual * precond_r),
                    jnp.sum(precond_r * image_z),
                    jnp.sum(precond_r * image_vec),
                    jnp.sum(direction * image_z),
                ]
            )
        ]
        if more:
            parts.append(local_means(image_z))
        sums = device_rows(jnp.concatenate(parts), every)
        fresh_rz = jnp.sum(sums[:, 0])
        ratio = fresh_rz / rz_now
        curvature = (
            jnp.sum(sums[:, 1])
            + ratio * (jnp.sum(sums[:, 2]) + jnp.sum(sums[:, 3]))
            + ratio * ratio * curvature
        )
        rz_now = fresh_rz
        direction = precond_r + ratio * direction
        image_vec = image_z + ratio * image_vec
        step_size = rz_now / curvature
        if more:
            image_means = sums[:, 4:].reshape(-1) + ratio * image_means
        displacement = displacement + step_size * direction
        residual = residual - step_size * image_vec
    return (displacement, residual)


def solution(mesh):
    return jax.shard_map(
        on_device,
        mesh=mesh,
        in_specs=(
            P(None, "slab", "col", None),
            P(None, "slab", "col", None),
            P("slab", "col", None),
            P(("slab", "col"), None),
        ),
        out_specs=(P(None, "slab", "col", None), P(None, "slab", "col", None)),
        check_vma=False,
    )
```

```python
import jax
import jax.numpy as jnp
import numpy as np
from jax import lax
from jax.sharding import PartitionSpec as P

ITERS = 2


STIFFNESS = 0.6
PENALTY = 2.0
FOUNDATION = 1.0


def with_halo(x, sides, width, low=True, high=True):
    for axis, dim in sides:
        count, length = (lax.axis_size(axis), x.shape[dim])
        up = [(i, (i + 1) % count) for i in range(count - 1)]
        down = [(j, i) for i, j in up]
        last = lax.slice_in_dim(x, length - width, length, axis=dim)
        first = lax.slice_in_dim(x, 0, width, axis=dim)
        parts = [x]
        if low:
            parts.insert(0, lax.ppermute(last, axis, up))
        if high:
            parts.append(lax.ppermute(first, axis, down))
        x = jnp.concatenate(parts, axis=dim)
    return x


def lower_rows(levels, reach, width):
    count, length = (lax.axis_size("slab"), levels.shape[1])
    up = [(i, i + 1) for i in range(count - 1)]
    starts = [int(np.argmax(reach >= depth)) for depth in range(1, width + 1)]
    sent = jnp.concatenate(
        [levels[start:, length - depth] for depth, start in zip(range(1, width + 1), starts)], axis=0
    )
    got = lax.ppermute(sent, "slab", up)
    rows, at = ({}, 0)
    for depth, start in zip(range(1, width + 1), starts):
        size = levels.shape[0] - start
        rows[depth] = jnp.concatenate(
            [jnp.zeros((start,) + levels.shape[2:], levels.dtype), got[at : at + size]], axis=0
        )
        at = at + size
    return jnp.stack([rows[depth] for depth in range(width, 0, -1)], axis=1)


def device_rows(vector, axes):
    count = 1
    for axis in axes:
        count = count * lax.axis_size(axis)
    tiled = jnp.broadcast_to(vector[None], (count,) + vector.shape)
    return lax.all_to_all(tiled, axes, 0, 0, tiled=True)


def bond_list():
    listed = []
    for shift_x in range(-3, 4):
        for shift_y in range(-3, 4):
            for shift_z in range(-3, 4):
                radius = shift_x * shift_x + shift_y * shift_y + shift_z * shift_z
                if 0 < radius <= 9 and (shift_x, shift_y, shift_z) > (0, 0, 0):
                    listed.append((shift_x, shift_y, shift_z))
    return listed


def bond_tables():
    offsets = np.array(bond_list(), dtype=np.int32)
    lengths = np.sqrt(np.sum(offsets * offsets, axis=1).astype(np.float32)).astype(np.float32)
    unit_dirs = (offsets.astype(np.float32) / lengths[:, None]).astype(np.float32)
    weights = (np.float32(STIFFNESS) / lengths).astype(np.float32)
    nearest = (lengths < 1.5).astype(np.float32)
    return (offsets, unit_dirs, weights, nearest)


def rim_mask(count, whole, position):
    places = position * count + jnp.arange(count + 6, dtype=jnp.int32) - 3
    return ((places >= 0) & (places < whole)).astype(jnp.float32)


def window(array, shift_x, shift_y, shift_z, extent):
    return array[
        ...,
        3 + shift_x : 3 + shift_x + extent[0],
        3 + shift_y : 3 + shift_y + extent[1],
        3 + shift_z : 3 + shift_z + extent[2],
    ]


def pad_depth(array):
    return jnp.pad(array, [(0, 0)] * (array.ndim - 1) + [(3, 3)])


def on_device(rhs_force, integrity, contact, coarse_inverse):
    components, cells_x, cells_y, depth = rhs_force.shape
    bond_count = integrity.shape[0]
    aggregates = coarse_inverse.shape[0] // 3
    agg_depth = depth // aggregates
    agg_cells = cells_x * cells_y * agg_depth
    extent = (cells_x, cells_y, depth)
    offsets, unit_dirs, weights, nearest = bond_tables()
    slab_mask = rim_mask(cells_x, cells_x * lax.axis_size("slab"), lax.axis_index("slab"))
    col_mask = rim_mask(cells_y, cells_y * lax.axis_size("col"), lax.axis_index("col"))
    depth_mask = rim_mask(depth, depth, jnp.zeros((), jnp.int32))
    inside_pad = slab_mask[:, None, None] * col_mask[None, :, None] * depth_mask[None, None, :]

    def bond_shift(bond_index):
        return [int(entry) for entry in offsets[bond_index]]

    def heading_of(bond_index):
        return [float(unit_dirs[bond_index, component]) for component in range(3)]

    def rimmed(vector):
        return pad_depth(with_halo(vector, (("col", 2), ("slab", 1)), 3))

    lower_x = jnp.concatenate([lower_rows(integrity, offsets[:, 0], 3), integrity], axis=1)
    spread = pad_depth(with_halo(lower_x, (("col", 2),), 3))
    contact_pad = pad_depth(
        with_halo(contact.astype(jnp.bfloat16), (("slab", 0), ("col", 1)), 3)
    ).astype(jnp.float32)
    near_contact = window(contact_pad, 0, 0, 0, extent)

    def bond_pair(bond_index):
        shift_x, shift_y, shift_z = bond_shift(bond_index)
        weight = float(weights[bond_index])
        level_pad = jnp.pad(spread[bond_index], ((0, 3), (0, 0), (0, 0)))
        intact = window(level_pad, 0, 0, 0, extent).astype(jnp.float32)
        prior = window(level_pad, -shift_x, -shift_y, -shift_z, extent).astype(jnp.float32)
        forward = weight * intact
        backward = weight * prior
        if nearest[bond_index] > 0.5:
            forward = forward + PENALTY * near_contact * window(
                contact_pad, shift_x, shift_y, shift_z, extent
            ) * (1.0 - intact)
            backward = backward + PENALTY * window(
                contact_pad, -shift_x, -shift_y, -shift_z, extent
            ) * near_contact * (1.0 - prior)
        forward = window(inside_pad, shift_x, shift_y, shift_z, extent) * forward
        return (forward, backward)

    diag_list = [jnp.full(extent, FOUNDATION, jnp.float32) for component in range(3)]
    for bond_index in range(bond_count):
        forward, backward = bond_pair(bond_index)
        heading = heading_of(bond_index)
        both_ends = forward + backward
        for component in range(3):
            diag_list[component] = (
                diag_list[component] + heading[component] * heading[component] * both_ends
            )
    diagonal = jnp.stack(diag_list)

    def operator(vector):
        padded = rimmed(vector)
        summed = [FOUNDATION * vector[component] for component in range(3)]
        for bond_index in range(bond_count):
            shift_x, shift_y, shift_z = bond_shift(bond_index)
            forward, backward = bond_pair(bond_index)
            heading = heading_of(bond_index)
            ahead_part = heading[0] * (
                vector[0] - window(padded[0], shift_x, shift_y, shift_z, extent)
            )
            behind_part = heading[0] * (
                vector[0] - window(padded[0], -shift_x, -shift_y, -shift_z, extent)
            )
            for component in range(1, 3):
                ahead_part = ahead_part + heading[component] * (
                    vector[component] - window(padded[component], shift_x, shift_y, shift_z, extent)
                )
                behind_part = behind_part + heading[component] * (
                    vector[component]
                    - window(padded[component], -shift_x, -shift_y, -shift_z, extent)
                )
            stretch = forward * ahead_part + backward * behind_part
            for component in range(3):
                summed[component] = summed[component] + heading[component] * stretch
        return jnp.stack(summed)

    def local_means(vector):
        blocks = vector.reshape(3, cells_x * cells_y, aggregates, agg_depth)
        return (jnp.sum(blocks, axis=(1, 3)) / agg_cells).T.reshape(3 * aggregates)

    def precondition(vector, coarse):
        solved = jnp.dot(coarse_inverse, coarse, precision=lax.Precision.HIGHEST)
        spread_back = solved.reshape(aggregates, 3).T[:, None, :, None]
        scaled = (vector / diagonal).reshape(
            3, cells_x * cells_y, aggregates, agg_depth
        ) + spread_back
        return scaled.reshape(vector.shape)

    every = ("slab", "col")

    residual = rhs_force
    coarse_now = device_rows(local_means(residual), every).reshape(-1)
    direction = precondition(residual, coarse_now)
    image_vec = operator(direction)
    sums = device_rows(
        jnp.concatenate(
            [
                jnp.stack([jnp.sum(residual * direction), jnp.sum(direction * image_vec)]),
                local_means(image_vec),
            ]
        ),
        every,
    )
    rz_now = jnp.sum(sums[:, 0])
    curvature = jnp.sum(sums[:, 1])
    step_size = rz_now / curvature
    image_means = sums[:, 2:].reshape(-1)
    displacement = step_size * direction
    residual = residual - step_size * image_vec
    for iteration in range(1, ITERS):
        more = iteration + 1 < ITERS
        coarse_now = coarse_now - step_size * image_means
        precond_r = precondition(residual, coarse_now)
        image_z = operator(precond_r)
        parts = [
            jnp.stack(
                [
                    jnp.sum(residual * precond_r),
                    jnp.sum(precond_r * image_z),
                    jnp.sum(precond_r * image_vec),
                    jnp.sum(direction * image_z),
                ]
            )
        ]
        if more:
            parts.append(local_means(image_z))
        sums = device_rows(jnp.concatenate(parts), every)
        fresh_rz = jnp.sum(sums[:, 0])
        ratio = fresh_rz / rz_now
        curvature = (
            jnp.sum(sums[:, 1])
            + ratio * (jnp.sum(sums[:, 2]) + jnp.sum(sums[:, 3]))
            + ratio * ratio * curvature
        )
        rz_now = fresh_rz
        direction = precond_r + ratio * direction
        image_vec = image_z + ratio * image_vec
        step_size = rz_now / curvature
        if more:
            image_means = sums[:, 4:].reshape(-1) + ratio * image_means
        displacement = displacement + step_size * direction
        residual = residual - step_size * image_vec
    return (displacement, residual)


def solution(mesh):
    return jax.shard_map(
        on_device,
        mesh=mesh,
        in_specs=(
            P(None, "slab", "col", None),
            P(None, "slab", "col", None),
            P("slab", "col", None),
            P(("slab", "col"), None),
        ),
        out_specs=(P(None, "slab", "col", None), P(None, "slab", "col", None)),
        check_vma=False,
    )
```

```python
import jax
import jax.numpy as jnp
import numpy as np
from jax import lax
from jax.sharding import PartitionSpec as P

ITERS = 2


STIFFNESS = 0.6
PENALTY = 2.0
FOUNDATION = 1.0


def with_halo(x, sides, width, low=True, high=True):
    for axis, dim in sides:
        count, length = (lax.axis_size(axis), x.shape[dim])
        up = [(i, (i + 1) % count) for i in range(count - 1)]
        down = [(j, i) for i, j in up]
        last = lax.slice_in_dim(x, length - width, length, axis=dim)
        first = lax.slice_in_dim(x, 0, width, axis=dim)
        parts = [x]
        if low:
            parts.insert(0, lax.ppermute(last, axis, up))
        if high:
            parts.append(lax.ppermute(first, axis, down))
        x = jnp.concatenate(parts, axis=dim)
    return x


def lower_rows(levels, reach, width, flags):
    count, length = (lax.axis_size("slab"), levels.shape[1])
    up = [(i, i + 1) for i in range(count - 1)]
    down = [(j, i) for i, j in up]
    starts = [int(np.argmax(reach >= depth)) for depth in range(1, width + 1)]
    sent = jnp.concatenate(
        [levels[start:, length - depth] for depth, start in zip(range(1, width + 1), starts)]
        + [flags[length - 1 :]],
        axis=0,
    )
    got = lax.ppermute(sent, "slab", up)
    above = lax.ppermute(flags[:1], "slab", down)
    plane = levels.shape[2:]
    rows, at = ({}, 0)
    for depth, start in zip(range(1, width + 1), starts):
        size = levels.shape[0] - start
        rows[depth] = jnp.concatenate(
            [jnp.zeros((start,) + plane, levels.dtype), got[at : at + size]], axis=0
        )
        at = at + size
    below = jnp.stack([rows[depth] for depth in range(width, 0, -1)], axis=1)
    bonds = jnp.concatenate(
        [below, levels, jnp.zeros((levels.shape[0], 1) + plane, levels.dtype)], axis=1
    )
    contact_rows = jnp.concatenate(
        [jnp.zeros((width - 1,) + plane, flags.dtype), got[at:], flags, above], axis=0
    )
    return jnp.concatenate([bonds, contact_rows[None]], axis=0)


def device_rows(vector, axes):
    count = 1
    for axis in axes:
        count = count * lax.axis_size(axis)
    tiled = jnp.broadcast_to(vector[None], (count,) + vector.shape)
    return lax.all_to_all(tiled, axes, 0, 0, tiled=True)


def bond_list():
    listed = []
    for shift_x in range(-3, 4):
        for shift_y in range(-3, 4):
            for shift_z in range(-3, 4):
                radius = shift_x * shift_x + shift_y * shift_y + shift_z * shift_z
                if 0 < radius <= 9 and (shift_x, shift_y, shift_z) > (0, 0, 0):
                    listed.append((shift_x, shift_y, shift_z))
    return listed


def bond_tables():
    offsets = np.array(bond_list(), dtype=np.int32)
    lengths = np.sqrt(np.sum(offsets * offsets, axis=1).astype(np.float32)).astype(np.float32)
    unit_dirs = (offsets.astype(np.float32) / lengths[:, None]).astype(np.float32)
    weights = (np.float32(STIFFNESS) / lengths).astype(np.float32)
    nearest = (lengths < 1.5).astype(np.float32)
    return (offsets, unit_dirs, weights, nearest)


def rim_mask(count, whole, position):
    places = position * count + jnp.arange(count + 6, dtype=jnp.int32) - 3
    return ((places >= 0) & (places < whole)).astype(jnp.float32)


def window(array, shift_x, shift_y, shift_z, extent):
    return array[
        ...,
        3 + shift_x : 3 + shift_x + extent[0],
        3 + shift_y : 3 + shift_y + extent[1],
        3 + shift_z : 3 + shift_z + extent[2],
    ]


def pad_depth(array):
    return jnp.pad(array, [(0, 0)] * (array.ndim - 1) + [(3, 3)])


def on_device(rhs_force, integrity, contact, coarse_inverse):
    components, cells_x, cells_y, depth = rhs_force.shape
    bond_count = integrity.shape[0]
    aggregates = coarse_inverse.shape[0] // 3
    agg_depth = depth // aggregates
    agg_cells = cells_x * cells_y * agg_depth
    extent = (cells_x, cells_y, depth)
    offsets, unit_dirs, weights, nearest = bond_tables()
    slab_mask = rim_mask(cells_x, cells_x * lax.axis_size("slab"), lax.axis_index("slab"))
    col_mask = rim_mask(cells_y, cells_y * lax.axis_size("col"), lax.axis_index("col"))
    depth_mask = rim_mask(depth, depth, jnp.zeros((), jnp.int32))
    inside_pad = slab_mask[:, None, None] * col_mask[None, :, None] * depth_mask[None, None, :]

    def bond_shift(bond_index):
        return [int(entry) for entry in offsets[bond_index]]

    def heading_of(bond_index):
        return [float(unit_dirs[bond_index, component]) for component in range(3)]

    def rimmed(vector):
        return pad_depth(with_halo(vector, (("slab", 1), ("col", 2)), 3))

    lower_x = lower_rows(integrity, offsets[:, 0], 3, contact.astype(jnp.bfloat16))
    spread = jnp.pad(
        pad_depth(with_halo(lower_x, (("col", 2),), 3)), ((0, 0), (0, 2), (0, 0), (0, 0))
    )
    contact_pad = spread[bond_count].astype(jnp.float32)
    near_contact = window(contact_pad, 0, 0, 0, extent)

    def bond_pair(bond_index):
        shift_x, shift_y, shift_z = bond_shift(bond_index)
        weight = float(weights[bond_index])
        level_pad = spread[bond_index]
        intact = window(level_pad, 0, 0, 0, extent).astype(jnp.float32)
        prior = window(level_pad, -shift_x, -shift_y, -shift_z, extent).astype(jnp.float32)
        forward = weight * intact
        backward = weight * prior
        if nearest[bond_index] > 0.5:
            forward = forward + PENALTY * near_contact * window(
                contact_pad, shift_x, shift_y, shift_z, extent
            ) * (1.0 - intact)
            backward = backward + PENALTY * window(
                contact_pad, -shift_x, -shift_y, -shift_z, extent
            ) * near_contact * (1.0 - prior)
        forward = window(inside_pad, shift_x, shift_y, shift_z, extent) * forward
        return (forward, backward)

    diag_list = [jnp.full(extent, FOUNDATION, jnp.float32) for component in range(3)]
    for bond_index in range(bond_count):
        forward, backward = bond_pair(bond_index)
        heading = heading_of(bond_index)
        both_ends = forward + backward
        for component in range(3):
            diag_list[component] = (
                diag_list[component] + heading[component] * heading[component] * both_ends
            )
    diagonal = jnp.stack(diag_list)

    def operator(vector):
        padded = rimmed(vector)
        summed = [FOUNDATION * vector[component] for component in range(3)]
        for bond_index in range(bond_count):
            shift_x, shift_y, shift_z = bond_shift(bond_index)
            forward, backward = bond_pair(bond_index)
            heading = heading_of(bond_index)
            ahead_part = heading[0] * (
                vector[0] - window(padded[0], shift_x, shift_y, shift_z, extent)
            )
            behind_part = heading[0] * (
                vector[0] - window(padded[0], -shift_x, -shift_y, -shift_z, extent)
            )
            for component in range(1, 3):
                ahead_part = ahead_part + heading[component] * (
                    vector[component] - window(padded[component], shift_x, shift_y, shift_z, extent)
                )
                behind_part = behind_part + heading[component] * (
                    vector[component]
                    - window(padded[component], -shift_x, -shift_y, -shift_z, extent)
                )
            stretch = forward * ahead_part + backward * behind_part
            for component in range(3):
                summed[component] = summed[component] + heading[component] * stretch
        return jnp.stack(summed)

    def local_means(vector):
        blocks = vector.reshape(3, cells_x * cells_y, aggregates, agg_depth)
        return (jnp.sum(blocks, axis=(1, 3)) / agg_cells).T.reshape(3 * aggregates)

    def precondition(vector, coarse):
        solved = jnp.dot(coarse_inverse, coarse, precision=lax.Precision.HIGHEST)
        spread_back = solved.reshape(aggregates, 3).T[:, None, :, None]
        scaled = (vector / diagonal).reshape(
            3, cells_x * cells_y, aggregates, agg_depth
        ) + spread_back
        return scaled.reshape(vector.shape)

    every = ("slab", "col")

    residual = rhs_force
    coarse_now = device_rows(local_means(residual), every).reshape(-1)
    direction = precondition(residual, coarse_now)
    image_vec = operator(direction)
    sums = device_rows(
        jnp.concatenate(
            [
                jnp.stack([jnp.sum(residual * direction), jnp.sum(direction * image_vec)]),
                local_means(image_vec),
            ]
        ),
        every,
    )
    rz_now = jnp.sum(sums[:, 0])
    curvature = jnp.sum(sums[:, 1])
    step_size = rz_now / curvature
    image_means = sums[:, 2:].reshape(-1)
    displacement = step_size * direction
    residual = residual - step_size * image_vec
    for iteration in range(1, ITERS):
        more = iteration + 1 < ITERS
        coarse_now = coarse_now - step_size * image_means
        precond_r = precondition(residual, coarse_now)
        image_z = operator(precond_r)
        parts = [
            jnp.stack(
                [
                    jnp.sum(residual * precond_r),
                    jnp.sum(precond_r * image_z),
                    jnp.sum(precond_r * image_vec),
                    jnp.sum(direction * image_z),
                ]
            )
        ]
        if more:
            parts.append(local_means(image_z))
        sums = device_rows(jnp.concatenate(parts), every)
        fresh_rz = jnp.sum(sums[:, 0])
        ratio = fresh_rz / rz_now
        curvature = (
            jnp.sum(sums[:, 1])
            + ratio * (jnp.sum(sums[:, 2]) + jnp.sum(sums[:, 3]))
            + ratio * ratio * curvature
        )
        rz_now = fresh_rz
        direction = precond_r + ratio * direction
        image_vec = image_z + ratio * image_vec
        step_size = rz_now / curvature
        if more:
            image_means = sums[:, 4:].reshape(-1) + ratio * image_means
        displacement = displacement + step_size * direction
        residual = residual - step_size * image_vec
    return (displacement, residual)


def solution(mesh):
    return jax.shard_map(
        on_device,
        mesh=mesh,
        in_specs=(
            P(None, "slab", "col", None),
            P(None, "slab", "col", None),
            P("slab", "col", None),
            P(("slab", "col"), None),
        ),
        out_specs=(P(None, "slab", "col", None), P(None, "slab", "col", None)),
        check_vma=False,
    )
```

```python
import jax
import jax.numpy as jnp
import numpy as np
from jax import lax
from jax.sharding import PartitionSpec as P

ITERS = 2


STIFFNESS = 0.6
PENALTY = 2.0
FOUNDATION = 1.0


def with_halo(x, sides, width, low=True, high=True):
    for axis, dim in sides:
        count, length = (lax.axis_size(axis), x.shape[dim])
        up = [(i, (i + 1) % count) for i in range(count - 1)]
        down = [(j, i) for i, j in up]
        last = lax.slice_in_dim(x, length - width, length, axis=dim)
        first = lax.slice_in_dim(x, 0, width, axis=dim)
        parts = [x]
        if low:
            parts.insert(0, lax.ppermute(last, axis, up))
        if high:
            parts.append(lax.ppermute(first, axis, down))
        x = jnp.concatenate(parts, axis=dim)
    return x


def lower_rows(levels, reach, width, flags):
    count, length = (lax.axis_size("slab"), levels.shape[1])
    up = [(i, i + 1) for i in range(count - 1)]
    down = [(j, i) for i, j in up]
    starts = [int(np.argmax(reach >= depth)) for depth in range(1, width + 1)]
    sent = jnp.concatenate(
        [levels[start:, length - depth] for depth, start in zip(range(1, width + 1), starts)]
        + [flags[length - 1 :]],
        axis=0,
    )
    got = lax.ppermute(sent, "slab", up)
    above = lax.ppermute(flags[:1], "slab", down)
    plane = levels.shape[2:]
    rows, at = ({}, 0)
    for depth, start in zip(range(1, width + 1), starts):
        size = levels.shape[0] - start
        rows[depth] = jnp.concatenate(
            [jnp.zeros((start,) + plane, levels.dtype), got[at : at + size]], axis=0
        )
        at = at + size
    below = jnp.stack([rows[depth] for depth in range(width, 0, -1)], axis=1)
    bonds = jnp.concatenate(
        [below, levels, jnp.zeros((levels.shape[0], 1) + plane, levels.dtype)], axis=1
    )
    contact_rows = jnp.concatenate(
        [jnp.zeros((width - 1,) + plane, flags.dtype), got[at:], flags, above], axis=0
    )
    return jnp.concatenate([bonds, contact_rows[None]], axis=0)


def device_rows(vector, axes):
    count = 1
    for axis in axes:
        count = count * lax.axis_size(axis)
    tiled = jnp.broadcast_to(vector[None], (count,) + vector.shape)
    return lax.all_to_all(tiled, axes, 0, 0, tiled=True)


def bond_list():
    listed = []
    for shift_x in range(-3, 4):
        for shift_y in range(-3, 4):
            for shift_z in range(-3, 4):
                radius = shift_x * shift_x + shift_y * shift_y + shift_z * shift_z
                if 0 < radius <= 9 and (shift_x, shift_y, shift_z) > (0, 0, 0):
                    listed.append((shift_x, shift_y, shift_z))
    return listed


def bond_tables():
    offsets = np.array(bond_list(), dtype=np.int32)
    lengths = np.sqrt(np.sum(offsets * offsets, axis=1).astype(np.float32)).astype(np.float32)
    unit_dirs = (offsets.astype(np.float32) / lengths[:, None]).astype(np.float32)
    weights = (np.float32(STIFFNESS) / lengths).astype(np.float32)
    nearest = (lengths < 1.5).astype(np.float32)
    return (offsets, unit_dirs, weights, nearest)


def rim_mask(count, whole, position):
    places = position * count + jnp.arange(count + 6, dtype=jnp.int32) - 3
    return ((places >= 0) & (places < whole)).astype(jnp.float32)


def window(array, shift_x, shift_y, shift_z, extent):
    return array[
        ...,
        3 + shift_x : 3 + shift_x + extent[0],
        3 + shift_y : 3 + shift_y + extent[1],
        3 + shift_z : 3 + shift_z + extent[2],
    ]


def pad_depth(array):
    return jnp.pad(array, [(0, 0)] * (array.ndim - 1) + [(3, 3)])


def on_device(rhs_force, integrity, contact, coarse_inverse):
    components, cells_x, cells_y, depth = rhs_force.shape
    bond_count = integrity.shape[0]
    aggregates = coarse_inverse.shape[0] // 3
    agg_depth = depth // aggregates
    agg_cells = cells_x * cells_y * agg_depth
    extent = (cells_x, cells_y, depth)
    offsets, unit_dirs, weights, nearest = bond_tables()
    slab_mask = rim_mask(cells_x, cells_x * lax.axis_size("slab"), lax.axis_index("slab"))
    col_mask = rim_mask(cells_y, cells_y * lax.axis_size("col"), lax.axis_index("col"))
    depth_mask = rim_mask(depth, depth, jnp.zeros((), jnp.int32))
    inside_pad = slab_mask[:, None, None] * col_mask[None, :, None] * depth_mask[None, None, :]

    def bond_shift(bond_index):
        return [int(entry) for entry in offsets[bond_index]]

    def heading_of(bond_index):
        return [float(unit_dirs[bond_index, component]) for component in range(3)]

    def rimmed(vector):
        return pad_depth(with_halo(vector, (("slab", 1), ("col", 2)), 3))

    lower_x = lower_rows(integrity, offsets[:, 0], 3, contact.astype(jnp.bfloat16))
    load_blocks = rhs_force.reshape(3, cells_x * cells_y, aggregates, agg_depth)
    load_means = (jnp.sum(load_blocks, axis=(1, 3)) / agg_cells).T.reshape(3 * aggregates)
    first_coarse = device_rows(load_means, ("slab", "col")).reshape(-1)
    first_coarse, lower_x = lax.optimization_barrier((first_coarse, lower_x))
    spread = jnp.pad(
        pad_depth(with_halo(lower_x, (("col", 2),), 3)), ((0, 0), (0, 2), (0, 0), (0, 0))
    )
    contact_pad = spread[bond_count].astype(jnp.float32)
    near_contact = window(contact_pad, 0, 0, 0, extent)

    def bond_pair(bond_index):
        shift_x, shift_y, shift_z = bond_shift(bond_index)
        weight = float(weights[bond_index])
        level_pad = spread[bond_index]
        intact = window(level_pad, 0, 0, 0, extent).astype(jnp.float32)
        prior = window(level_pad, -shift_x, -shift_y, -shift_z, extent).astype(jnp.float32)
        forward = weight * intact
        backward = weight * prior
        if nearest[bond_index] > 0.5:
            forward = forward + PENALTY * near_contact * window(
                contact_pad, shift_x, shift_y, shift_z, extent
            ) * (1.0 - intact)
            backward = backward + PENALTY * window(
                contact_pad, -shift_x, -shift_y, -shift_z, extent
            ) * near_contact * (1.0 - prior)
        forward = window(inside_pad, shift_x, shift_y, shift_z, extent) * forward
        return (forward, backward)

    diag_list = [jnp.full(extent, FOUNDATION, jnp.float32) for component in range(3)]
    for bond_index in range(bond_count):
        forward, backward = bond_pair(bond_index)
        heading = heading_of(bond_index)
        both_ends = forward + backward
        for component in range(3):
            diag_list[component] = (
                diag_list[component] + heading[component] * heading[component] * both_ends
            )
    diagonal = jnp.stack(diag_list)

    def operator(vector):
        padded = rimmed(vector)
        summed = [FOUNDATION * vector[component] for component in range(3)]
        for bond_index in range(bond_count):
            shift_x, shift_y, shift_z = bond_shift(bond_index)
            forward, backward = bond_pair(bond_index)
            heading = heading_of(bond_index)
            ahead_part = heading[0] * (
                vector[0] - window(padded[0], shift_x, shift_y, shift_z, extent)
            )
            behind_part = heading[0] * (
                vector[0] - window(padded[0], -shift_x, -shift_y, -shift_z, extent)
            )
            for component in range(1, 3):
                ahead_part = ahead_part + heading[component] * (
                    vector[component] - window(padded[component], shift_x, shift_y, shift_z, extent)
                )
                behind_part = behind_part + heading[component] * (
                    vector[component]
                    - window(padded[component], -shift_x, -shift_y, -shift_z, extent)
                )
            stretch = forward * ahead_part + backward * behind_part
            for component in range(3):
                summed[component] = summed[component] + heading[component] * stretch
        return jnp.stack(summed)

    def local_means(vector):
        blocks = vector.reshape(3, cells_x * cells_y, aggregates, agg_depth)
        return (jnp.sum(blocks, axis=(1, 3)) / agg_cells).T.reshape(3 * aggregates)

    def precondition(vector, coarse):
        solved = jnp.dot(coarse_inverse, coarse, precision=lax.Precision.HIGHEST)
        spread_back = solved.reshape(aggregates, 3).T[:, None, :, None]
        scaled = (vector / diagonal).reshape(
            3, cells_x * cells_y, aggregates, agg_depth
        ) + spread_back
        return scaled.reshape(vector.shape)

    every = ("slab", "col")

    residual = rhs_force
    coarse_now = first_coarse
    direction = precondition(residual, coarse_now)
    image_vec = operator(direction)
    sums = device_rows(
        jnp.concatenate(
            [
                jnp.stack([jnp.sum(residual * direction), jnp.sum(direction * image_vec)]),
                local_means(image_vec),
            ]
        ),
        every,
    )
    rz_now = jnp.sum(sums[:, 0])
    curvature = jnp.sum(sums[:, 1])
    step_size = rz_now / curvature
    image_means = sums[:, 2:].reshape(-1)
    displacement = step_size * direction
    residual = residual - step_size * image_vec
    for iteration in range(1, ITERS):
        more = iteration + 1 < ITERS
        coarse_now = coarse_now - step_size * image_means
        precond_r = precondition(residual, coarse_now)
        image_z = operator(precond_r)
        parts = [
            jnp.stack(
                [
                    jnp.sum(residual * precond_r),
                    jnp.sum(precond_r * image_z),
                    jnp.sum(precond_r * image_vec),
                    jnp.sum(direction * image_z),
                ]
            )
        ]
        if more:
            parts.append(local_means(image_z))
        sums = device_rows(jnp.concatenate(parts), every)
        fresh_rz = jnp.sum(sums[:, 0])
        ratio = fresh_rz / rz_now
        curvature = (
            jnp.sum(sums[:, 1])
            + ratio * (jnp.sum(sums[:, 2]) + jnp.sum(sums[:, 3]))
            + ratio * ratio * curvature
        )
        rz_now = fresh_rz
        direction = precond_r + ratio * direction
        image_vec = image_z + ratio * image_vec
        step_size = rz_now / curvature
        if more:
            image_means = sums[:, 4:].reshape(-1) + ratio * image_means
        displacement = displacement + step_size * direction
        residual = residual - step_size * image_vec
    return (displacement, residual)


def solution(mesh):
    return jax.shard_map(
        on_device,
        mesh=mesh,
        in_specs=(
            P(None, "slab", "col", None),
            P(None, "slab", "col", None),
            P("slab", "col", None),
            P(("slab", "col"), None),
        ),
        out_specs=(P(None, "slab", "col", None), P(None, "slab", "col", None)),
        check_vma=False,
    )
```

```python
import jax
import jax.numpy as jnp
import numpy as np
from jax import lax
from jax.sharding import PartitionSpec as P

ITERS = 2


STIFFNESS = 0.6
PENALTY = 2.0
FOUNDATION = 1.0


def with_halo(x, sides, width, low=True, high=True):
    for axis, dim in sides:
        count, length = (lax.axis_size(axis), x.shape[dim])
        up = [(i, (i + 1) % count) for i in range(count - 1)]
        down = [(j, i) for i, j in up]
        last = lax.slice_in_dim(x, length - width, length, axis=dim)
        first = lax.slice_in_dim(x, 0, width, axis=dim)
        parts = [x]
        if low:
            parts.insert(0, lax.ppermute(last, axis, up))
        if high:
            parts.append(lax.ppermute(first, axis, down))
        x = jnp.concatenate(parts, axis=dim)
    return x


def lower_rows(levels, reach, width, flags):
    count, length = (lax.axis_size("slab"), levels.shape[1])
    up = [(i, i + 1) for i in range(count - 1)]
    down = [(j, i) for i, j in up]
    starts = [int(np.argmax(reach >= depth)) for depth in range(1, width + 1)]
    sent = jnp.concatenate(
        [levels[start:, length - depth] for depth, start in zip(range(1, width + 1), starts)]
        + [flags[length - 1 :]],
        axis=0,
    )
    got = lax.ppermute(sent, "slab", up)
    above = lax.ppermute(flags[:1], "slab", down)
    plane = levels.shape[2:]
    rows, at = ({}, 0)
    for depth, start in zip(range(1, width + 1), starts):
        size = levels.shape[0] - start
        rows[depth] = jnp.concatenate(
            [jnp.zeros((start,) + plane, levels.dtype), got[at : at + size]], axis=0
        )
        at = at + size
    below = jnp.stack([rows[depth] for depth in range(width, 0, -1)], axis=1)
    bonds = jnp.concatenate(
        [below, levels, jnp.zeros((levels.shape[0], 1) + plane, levels.dtype)], axis=1
    )
    contact_rows = jnp.concatenate(
        [jnp.zeros((width - 1,) + plane, flags.dtype), got[at:], flags, above], axis=0
    )
    return jnp.concatenate([bonds, contact_rows[None]], axis=0)


def device_rows(vector, axes):
    count = 1
    for axis in axes:
        count = count * lax.axis_size(axis)
    tiled = jnp.broadcast_to(vector[None], (count,) + vector.shape)
    return lax.all_to_all(tiled, axes, 0, 0, tiled=True)


def bond_list():
    listed = []
    for shift_x in range(-3, 4):
        for shift_y in range(-3, 4):
            for shift_z in range(-3, 4):
                radius = shift_x * shift_x + shift_y * shift_y + shift_z * shift_z
                if 0 < radius <= 9 and (shift_x, shift_y, shift_z) > (0, 0, 0):
                    listed.append((shift_x, shift_y, shift_z))
    return listed


def bond_tables():
    offsets = np.array(bond_list(), dtype=np.int32)
    lengths = np.sqrt(np.sum(offsets * offsets, axis=1).astype(np.float32)).astype(np.float32)
    unit_dirs = (offsets.astype(np.float32) / lengths[:, None]).astype(np.float32)
    weights = (np.float32(STIFFNESS) / lengths).astype(np.float32)
    nearest = (lengths < 1.5).astype(np.float32)
    return (offsets, unit_dirs, weights, nearest)


def rim_mask(count, whole, position):
    places = position * count + jnp.arange(count + 6, dtype=jnp.int32) - 3
    return ((places >= 0) & (places < whole)).astype(jnp.float32)


def window(array, shift_x, shift_y, shift_z, extent):
    return array[
        ...,
        3 + shift_x : 3 + shift_x + extent[0],
        3 + shift_y : 3 + shift_y + extent[1],
        3 + shift_z : 3 + shift_z + extent[2],
    ]


def pad_depth(array):
    return jnp.pad(array, [(0, 0)] * (array.ndim - 1) + [(3, 3)])


def on_device(rhs_force, integrity, contact, coarse_inverse):
    components, cells_x, cells_y, depth = rhs_force.shape
    bond_count = integrity.shape[0]
    aggregates = coarse_inverse.shape[0] // 3
    agg_depth = depth // aggregates
    agg_cells = cells_x * cells_y * agg_depth
    extent = (cells_x, cells_y, depth)
    offsets, unit_dirs, weights, nearest = bond_tables()
    slab_mask = rim_mask(cells_x, cells_x * lax.axis_size("slab"), lax.axis_index("slab"))
    col_mask = rim_mask(cells_y, cells_y * lax.axis_size("col"), lax.axis_index("col"))
    depth_mask = rim_mask(depth, depth, jnp.zeros((), jnp.int32))
    inside_pad = slab_mask[:, None, None] * col_mask[None, :, None] * depth_mask[None, None, :]

    def bond_shift(bond_index):
        return [int(entry) for entry in offsets[bond_index]]

    def heading_of(bond_index):
        return [float(unit_dirs[bond_index, component]) for component in range(3)]

    def rimmed(vector):
        return pad_depth(with_halo(vector, (("slab", 1), ("col", 2)), 3))

    lower_x = lower_rows(integrity, offsets[:, 0], 3, contact.astype(jnp.bfloat16))
    load_blocks = rhs_force.reshape(3, cells_x * cells_y, aggregates, agg_depth)
    load_means = (jnp.sum(load_blocks, axis=(1, 3)) / agg_cells).T.reshape(3 * aggregates)
    first_coarse = device_rows(load_means, ("slab", "col")).reshape(-1)
    first_coarse, lower_x = lax.optimization_barrier((first_coarse, lower_x))
    spread = jnp.pad(
        pad_depth(with_halo(lower_x, (("col", 2),), 3)), ((0, 0), (0, 2), (0, 0), (0, 0))
    )
    contact_pad = spread[bond_count].astype(jnp.float32)
    near_contact = window(contact_pad, 0, 0, 0, extent)

    def bond_pair(bond_index):
        shift_x, shift_y, shift_z = bond_shift(bond_index)
        weight = float(weights[bond_index])
        level_pad = spread[bond_index]
        intact = window(level_pad, 0, 0, 0, extent).astype(jnp.float32)
        prior = window(level_pad, -shift_x, -shift_y, -shift_z, extent).astype(jnp.float32)
        forward = weight * intact
        backward = weight * prior
        if nearest[bond_index] > 0.5:
            forward = forward + PENALTY * near_contact * window(
                contact_pad, shift_x, shift_y, shift_z, extent
            ) * (1.0 - intact)
            backward = backward + PENALTY * window(
                contact_pad, -shift_x, -shift_y, -shift_z, extent
            ) * near_contact * (1.0 - prior)
        forward = window(inside_pad, shift_x, shift_y, shift_z, extent) * forward
        return (forward, backward)

    diagonal = jnp.full((3,) + extent, FOUNDATION, jnp.float32)
    for bond_index in range(bond_count):
        forward, backward = bond_pair(bond_index)
        squares = np.array([entry * entry for entry in heading_of(bond_index)], np.float32)
        diagonal = diagonal + jnp.asarray(squares).reshape(3, 1, 1, 1) * (forward + backward)[None]

    def operator(vector):
        padded = rimmed(vector)
        summed = [FOUNDATION * vector[component] for component in range(3)]
        for bond_index in range(bond_count):
            shift_x, shift_y, shift_z = bond_shift(bond_index)
            forward, backward = bond_pair(bond_index)
            heading = heading_of(bond_index)
            ahead_part = heading[0] * (
                vector[0] - window(padded[0], shift_x, shift_y, shift_z, extent)
            )
            behind_part = heading[0] * (
                vector[0] - window(padded[0], -shift_x, -shift_y, -shift_z, extent)
            )
            for component in range(1, 3):
                ahead_part = ahead_part + heading[component] * (
                    vector[component] - window(padded[component], shift_x, shift_y, shift_z, extent)
                )
                behind_part = behind_part + heading[component] * (
                    vector[component]
                    - window(padded[component], -shift_x, -shift_y, -shift_z, extent)
                )
            stretch = forward * ahead_part + backward * behind_part
            for component in range(3):
                summed[component] = summed[component] + heading[component] * stretch
        return jnp.stack(summed)

    def local_means(vector):
        blocks = vector.reshape(3, cells_x * cells_y, aggregates, agg_depth)
        return (jnp.sum(blocks, axis=(1, 3)) / agg_cells).T.reshape(3 * aggregates)

    def precondition(vector, coarse):
        solved = jnp.dot(coarse_inverse, coarse, precision=lax.Precision.HIGHEST)
        spread_back = solved.reshape(aggregates, 3).T[:, None, :, None]
        scaled = (vector / diagonal).reshape(
            3, cells_x * cells_y, aggregates, agg_depth
        ) + spread_back
        return scaled.reshape(vector.shape)

    every = ("slab", "col")

    residual = rhs_force
    coarse_now = first_coarse
    direction = precondition(residual, coarse_now)
    image_vec = operator(direction)
    sums = device_rows(
        jnp.concatenate(
            [
                jnp.stack([jnp.sum(residual * direction), jnp.sum(direction * image_vec)]),
                local_means(image_vec),
            ]
        ),
        every,
    )
    rz_now = jnp.sum(sums[:, 0])
    curvature = jnp.sum(sums[:, 1])
    step_size = rz_now / curvature
    image_means = sums[:, 2:].reshape(-1)
    displacement = step_size * direction
    residual = residual - step_size * image_vec
    for iteration in range(1, ITERS):
        more = iteration + 1 < ITERS
        coarse_now = coarse_now - step_size * image_means
        precond_r = precondition(residual, coarse_now)
        image_z = operator(precond_r)
        parts = [
            jnp.stack(
                [
                    jnp.sum(residual * precond_r),
                    jnp.sum(precond_r * image_z),
                    jnp.sum(precond_r * image_vec),
                    jnp.sum(direction * image_z),
                ]
            )
        ]
        if more:
            parts.append(local_means(image_z))
        sums = device_rows(jnp.concatenate(parts), every)
        fresh_rz = jnp.sum(sums[:, 0])
        ratio = fresh_rz / rz_now
        curvature = (
            jnp.sum(sums[:, 1])
            + ratio * (jnp.sum(sums[:, 2]) + jnp.sum(sums[:, 3]))
            + ratio * ratio * curvature
        )
        rz_now = fresh_rz
        direction = precond_r + ratio * direction
        image_vec = image_z + ratio * image_vec
        step_size = rz_now / curvature
        if more:
            image_means = sums[:, 4:].reshape(-1) + ratio * image_means
        displacement = displacement + step_size * direction
        residual = residual - step_size * image_vec
    return (displacement, residual)


def solution(mesh):
    return jax.shard_map(
        on_device,
        mesh=mesh,
        in_specs=(
            P(None, "slab", "col", None),
            P(None, "slab", "col", None),
            P("slab", "col", None),
            P(("slab", "col"), None),
        ),
        out_specs=(P(None, "slab", "col", None), P(None, "slab", "col", None)),
        check_vma=False,
    )
```

```python
import jax
import jax.numpy as jnp
import numpy as np
from jax import lax
from jax.sharding import PartitionSpec as P

ITERS = 2


STIFFNESS = 0.6
PENALTY = 2.0
FOUNDATION = 1.0


def with_halo(x, sides, width, low=True, high=True):
    for axis, dim in sides:
        count, length = (lax.axis_size(axis), x.shape[dim])
        up = [(i, (i + 1) % count) for i in range(count - 1)]
        down = [(j, i) for i, j in up]
        last = lax.slice_in_dim(x, length - width, length, axis=dim)
        first = lax.slice_in_dim(x, 0, width, axis=dim)
        parts = [x]
        if low:
            parts.insert(0, lax.ppermute(last, axis, up))
        if high:
            parts.append(lax.ppermute(first, axis, down))
        x = jnp.concatenate(parts, axis=dim)
    return x


def lower_rows(levels, reach, width, flags):
    count, length = (lax.axis_size("slab"), levels.shape[1])
    up = [(i, i + 1) for i in range(count - 1)]
    down = [(j, i) for i, j in up]
    starts = [int(np.argmax(reach >= depth)) for depth in range(1, width + 1)]
    sent = jnp.concatenate(
        [levels[start:, length - depth] for depth, start in zip(range(1, width + 1), starts)]
        + [flags[length - 1 :]],
        axis=0,
    )
    got = lax.ppermute(sent, "slab", up)
    above = lax.ppermute(flags[:1], "slab", down)
    plane = levels.shape[2:]
    rows, at = ({}, 0)
    for depth, start in zip(range(1, width + 1), starts):
        size = levels.shape[0] - start
        rows[depth] = jnp.concatenate(
            [jnp.zeros((start,) + plane, levels.dtype), got[at : at + size]], axis=0
        )
        at = at + size
    below = jnp.stack([rows[depth] for depth in range(width, 0, -1)], axis=1)
    bonds = jnp.concatenate(
        [below, levels, jnp.zeros((levels.shape[0], 1) + plane, levels.dtype)], axis=1
    )
    contact_rows = jnp.concatenate(
        [jnp.zeros((width - 1,) + plane, flags.dtype), got[at:], flags, above], axis=0
    )
    return jnp.concatenate([bonds, contact_rows[None]], axis=0)


def device_rows(vector, axes):
    count = 1
    for axis in axes:
        count = count * lax.axis_size(axis)
    tiled = jnp.broadcast_to(vector[None], (count,) + vector.shape)
    return lax.all_to_all(tiled, axes, 0, 0, tiled=True)


def bond_list():
    listed = []
    for shift_x in range(-3, 4):
        for shift_y in range(-3, 4):
            for shift_z in range(-3, 4):
                radius = shift_x * shift_x + shift_y * shift_y + shift_z * shift_z
                if 0 < radius <= 9 and (shift_x, shift_y, shift_z) > (0, 0, 0):
                    listed.append((shift_x, shift_y, shift_z))
    return listed


def bond_tables():
    offsets = np.array(bond_list(), dtype=np.int32)
    lengths = np.sqrt(np.sum(offsets * offsets, axis=1).astype(np.float32)).astype(np.float32)
    unit_dirs = (offsets.astype(np.float32) / lengths[:, None]).astype(np.float32)
    weights = (np.float32(STIFFNESS) / lengths).astype(np.float32)
    nearest = (lengths < 1.5).astype(np.float32)
    return (offsets, unit_dirs, weights, nearest)


def rim_mask(count, whole, position):
    places = position * count + jnp.arange(count + 6, dtype=jnp.int32) - 3
    return ((places >= 0) & (places < whole)).astype(jnp.float32)


def window(array, shift_x, shift_y, shift_z, extent):
    return array[
        ...,
        3 + shift_x : 3 + shift_x + extent[0],
        3 + shift_y : 3 + shift_y + extent[1],
        3 + shift_z : 3 + shift_z + extent[2],
    ]


def pad_depth(array):
    return jnp.pad(array, [(0, 0)] * (array.ndim - 1) + [(3, 3)])


def on_device(rhs_force, integrity, contact, coarse_inverse):
    components, cells_x, cells_y, depth = rhs_force.shape
    bond_count = integrity.shape[0]
    aggregates = coarse_inverse.shape[0] // 3
    agg_depth = depth // aggregates
    agg_cells = cells_x * cells_y * agg_depth
    extent = (cells_x, cells_y, depth)
    offsets, unit_dirs, weights, nearest = bond_tables()
    slab_mask = rim_mask(cells_x, cells_x * lax.axis_size("slab"), lax.axis_index("slab"))
    col_mask = rim_mask(cells_y, cells_y * lax.axis_size("col"), lax.axis_index("col"))
    depth_mask = rim_mask(depth, depth, jnp.zeros((), jnp.int32))
    inside_pad = slab_mask[:, None, None] * col_mask[None, :, None] * depth_mask[None, None, :]

    def bond_shift(bond_index):
        return [int(entry) for entry in offsets[bond_index]]

    def heading_of(bond_index):
        return [float(unit_dirs[bond_index, component]) for component in range(3)]

    def rimmed(vector):
        return pad_depth(with_halo(vector, (("slab", 1), ("col", 2)), 3))

    lower_x = lower_rows(integrity, offsets[:, 0], 3, contact.astype(jnp.bfloat16))
    load_blocks = rhs_force.reshape(3, cells_x * cells_y, aggregates, agg_depth)
    load_means = (jnp.sum(load_blocks, axis=(1, 3)) / agg_cells).T.reshape(3 * aggregates)
    first_coarse = device_rows(load_means, ("slab", "col")).reshape(-1)
    first_coarse, lower_x = lax.optimization_barrier((first_coarse, lower_x))
    spread = jnp.pad(
        pad_depth(with_halo(lower_x, (("col", 2),), 3)), ((0, 0), (0, 2), (0, 0), (0, 0))
    )
    contact_pad = spread[bond_count].astype(jnp.float32)
    near_contact = window(contact_pad, 0, 0, 0, extent)

    def bond_pair(bond_index):
        shift_x, shift_y, shift_z = bond_shift(bond_index)
        weight = float(weights[bond_index])
        level_pad = spread[bond_index]
        intact = window(level_pad, 0, 0, 0, extent).astype(jnp.float32)
        prior = window(level_pad, -shift_x, -shift_y, -shift_z, extent).astype(jnp.float32)
        forward = weight * intact
        backward = weight * prior
        if nearest[bond_index] > 0.5:
            forward = forward + PENALTY * near_contact * window(
                contact_pad, shift_x, shift_y, shift_z, extent
            ) * (1.0 - intact)
            backward = backward + PENALTY * window(
                contact_pad, -shift_x, -shift_y, -shift_z, extent
            ) * near_contact * (1.0 - prior)
        forward = window(inside_pad, shift_x, shift_y, shift_z, extent) * forward
        return (forward, backward)

    diagonal = jnp.full((3,) + extent, FOUNDATION, jnp.float32)
    for bond_index in range(bond_count):
        forward, backward = bond_pair(bond_index)
        squares = np.array([entry * entry for entry in heading_of(bond_index)], np.float32)
        diagonal = diagonal + jnp.asarray(squares).reshape(3, 1, 1, 1) * (forward + backward)[None]

    def operator(vector):
        padded = rimmed(vector)
        summed = FOUNDATION * vector
        for bond_index in range(bond_count):
            shift_x, shift_y, shift_z = bond_shift(bond_index)
            forward, backward = bond_pair(bond_index)
            heading = heading_of(bond_index)
            ahead_part = heading[0] * (
                vector[0] - window(padded[0], shift_x, shift_y, shift_z, extent)
            )
            behind_part = heading[0] * (
                vector[0] - window(padded[0], -shift_x, -shift_y, -shift_z, extent)
            )
            for component in range(1, 3):
                ahead_part = ahead_part + heading[component] * (
                    vector[component] - window(padded[component], shift_x, shift_y, shift_z, extent)
                )
                behind_part = behind_part + heading[component] * (
                    vector[component]
                    - window(padded[component], -shift_x, -shift_y, -shift_z, extent)
                )
            stretch = forward * ahead_part + backward * behind_part
            headings = jnp.asarray(np.array(heading, np.float32)).reshape(3, 1, 1, 1)
            summed = summed + headings * stretch[None]
        return summed

    def local_means(vector):
        blocks = vector.reshape(3, cells_x * cells_y, aggregates, agg_depth)
        return (jnp.sum(blocks, axis=(1, 3)) / agg_cells).T.reshape(3 * aggregates)

    def precondition(vector, coarse):
        solved = jnp.dot(coarse_inverse, coarse, precision=lax.Precision.HIGHEST)
        spread_back = solved.reshape(aggregates, 3).T[:, None, :, None]
        scaled = (vector / diagonal).reshape(
            3, cells_x * cells_y, aggregates, agg_depth
        ) + spread_back
        return scaled.reshape(vector.shape)

    every = ("slab", "col")

    residual = rhs_force
    coarse_now = first_coarse
    direction = precondition(residual, coarse_now)
    image_vec = operator(direction)
    sums = device_rows(
        jnp.concatenate(
            [
                jnp.stack([jnp.sum(residual * direction), jnp.sum(direction * image_vec)]),
                local_means(image_vec),
            ]
        ),
        every,
    )
    rz_now = jnp.sum(sums[:, 0])
    curvature = jnp.sum(sums[:, 1])
    step_size = rz_now / curvature
    image_means = sums[:, 2:].reshape(-1)
    displacement = step_size * direction
    residual = residual - step_size * image_vec
    for iteration in range(1, ITERS):
        more = iteration + 1 < ITERS
        coarse_now = coarse_now - step_size * image_means
        precond_r = precondition(residual, coarse_now)
        image_z = operator(precond_r)
        parts = [
            jnp.stack(
                [
                    jnp.sum(residual * precond_r),
                    jnp.sum(precond_r * image_z),
                    jnp.sum(precond_r * image_vec),
                    jnp.sum(direction * image_z),
                ]
            )
        ]
        if more:
            parts.append(local_means(image_z))
        sums = device_rows(jnp.concatenate(parts), every)
        fresh_rz = jnp.sum(sums[:, 0])
        ratio = fresh_rz / rz_now
        curvature = (
            jnp.sum(sums[:, 1])
            + ratio * (jnp.sum(sums[:, 2]) + jnp.sum(sums[:, 3]))
            + ratio * ratio * curvature
        )
        rz_now = fresh_rz
        direction = precond_r + ratio * direction
        image_vec = image_z + ratio * image_vec
        step_size = rz_now / curvature
        if more:
            image_means = sums[:, 4:].reshape(-1) + ratio * image_means
        displacement = displacement + step_size * direction
        residual = residual - step_size * image_vec
    return (displacement, residual)


def solution(mesh):
    return jax.shard_map(
        on_device,
        mesh=mesh,
        in_specs=(
            P(None, "slab", "col", None),
            P(None, "slab", "col", None),
            P("slab", "col", None),
            P(("slab", "col"), None),
        ),
        out_specs=(P(None, "slab", "col", None), P(None, "slab", "col", None)),
        check_vma=False,
    )
```

```python
import jax
import jax.numpy as jnp
import numpy as np
from jax import lax
from jax.sharding import PartitionSpec as P

ITERS = 2


STIFFNESS = 0.6
PENALTY = 2.0
FOUNDATION = 1.0


def with_halo(x, sides, width, low=True, high=True, whole=False):
    for axis, dim in sides:
        count, length = (lax.axis_size(axis), x.shape[dim])
        up = [(i, (i + 1) % count) for i in range(count - 1)]
        down = [(j, i) for i, j in up]
        last = x if whole else lax.slice_in_dim(x, length - width, length, axis=dim)
        first = x if whole else lax.slice_in_dim(x, 0, width, axis=dim)
        parts = [x]
        if low:
            below = lax.ppermute(last, axis, up)
            if whole:
                below = lax.slice_in_dim(below, length - width, length, axis=dim)
            parts.insert(0, below)
        if high:
            above = lax.ppermute(first, axis, down)
            if whole:
                above = lax.slice_in_dim(above, 0, width, axis=dim)
            parts.append(above)
        x = jnp.concatenate(parts, axis=dim)
    return x


def lower_rows(levels, reach, width, flags):
    count, length = (lax.axis_size("slab"), levels.shape[1])
    up = [(i, i + 1) for i in range(count - 1)]
    down = [(j, i) for i, j in up]
    starts = [int(np.argmax(reach >= depth)) for depth in range(1, width + 1)]
    sent = jnp.concatenate(
        [levels[start:, length - depth] for depth, start in zip(range(1, width + 1), starts)]
        + [flags[length - 1 :]],
        axis=0,
    )
    got = lax.ppermute(sent, "slab", up)
    above = lax.ppermute(flags[:1], "slab", down)
    plane = levels.shape[2:]
    rows, at = ({}, 0)
    for depth, start in zip(range(1, width + 1), starts):
        size = levels.shape[0] - start
        rows[depth] = jnp.concatenate(
            [jnp.zeros((start,) + plane, levels.dtype), got[at : at + size]], axis=0
        )
        at = at + size
    below = jnp.stack([rows[depth] for depth in range(width, 0, -1)], axis=1)
    bonds = jnp.concatenate(
        [below, levels, jnp.zeros((levels.shape[0], 1) + plane, levels.dtype)], axis=1
    )
    contact_rows = jnp.concatenate(
        [jnp.zeros((width - 1,) + plane, flags.dtype), got[at:], flags, above], axis=0
    )
    return jnp.concatenate([bonds, contact_rows[None]], axis=0)


def device_rows(vector, axes):
    count = 1
    for axis in axes:
        count = count * lax.axis_size(axis)
    tiled = jnp.broadcast_to(vector[None], (count,) + vector.shape)
    return lax.all_to_all(tiled, axes, 0, 0, tiled=True)


def bond_list():
    listed = []
    for shift_x in range(-3, 4):
        for shift_y in range(-3, 4):
            for shift_z in range(-3, 4):
                radius = shift_x * shift_x + shift_y * shift_y + shift_z * shift_z
                if 0 < radius <= 9 and (shift_x, shift_y, shift_z) > (0, 0, 0):
                    listed.append((shift_x, shift_y, shift_z))
    return listed


def bond_tables():
    offsets = np.array(bond_list(), dtype=np.int32)
    lengths = np.sqrt(np.sum(offsets * offsets, axis=1).astype(np.float32)).astype(np.float32)
    unit_dirs = (offsets.astype(np.float32) / lengths[:, None]).astype(np.float32)
    weights = (np.float32(STIFFNESS) / lengths).astype(np.float32)
    nearest = (lengths < 1.5).astype(np.float32)
    return (offsets, unit_dirs, weights, nearest)


def rim_mask(count, whole, position):
    places = position * count + jnp.arange(count + 6, dtype=jnp.int32) - 3
    return ((places >= 0) & (places < whole)).astype(jnp.float32)


def window(array, shift_x, shift_y, shift_z, extent):
    return array[
        ...,
        3 + shift_x : 3 + shift_x + extent[0],
        3 + shift_y : 3 + shift_y + extent[1],
        3 + shift_z : 3 + shift_z + extent[2],
    ]


def pad_depth(array):
    return jnp.pad(array, [(0, 0)] * (array.ndim - 1) + [(3, 3)])


def on_device(rhs_force, integrity, contact, coarse_inverse):
    components, cells_x, cells_y, depth = rhs_force.shape
    bond_count = integrity.shape[0]
    aggregates = coarse_inverse.shape[0] // 3
    agg_depth = depth // aggregates
    agg_cells = cells_x * cells_y * agg_depth
    extent = (cells_x, cells_y, depth)
    offsets, unit_dirs, weights, nearest = bond_tables()
    slab_mask = rim_mask(cells_x, cells_x * lax.axis_size("slab"), lax.axis_index("slab"))
    col_mask = rim_mask(cells_y, cells_y * lax.axis_size("col"), lax.axis_index("col"))
    depth_mask = rim_mask(depth, depth, jnp.zeros((), jnp.int32))
    inside_pad = slab_mask[:, None, None] * col_mask[None, :, None] * depth_mask[None, None, :]

    def bond_shift(bond_index):
        return [int(entry) for entry in offsets[bond_index]]

    def heading_of(bond_index):
        return [float(unit_dirs[bond_index, component]) for component in range(3)]

    def rimmed(vector):
        return pad_depth(with_halo(vector, (("slab", 1), ("col", 2)), 3))

    lower_x = lower_rows(integrity, offsets[:, 0], 3, contact.astype(jnp.bfloat16))
    load_blocks = rhs_force.reshape(3, cells_x * cells_y, aggregates, agg_depth)
    load_means = (jnp.sum(load_blocks, axis=(1, 3)) / agg_cells).T.reshape(3 * aggregates)
    first_coarse = device_rows(load_means, ("slab", "col")).reshape(-1)
    first_coarse, lower_x = lax.optimization_barrier((first_coarse, lower_x))
    spread = jnp.pad(
        pad_depth(with_halo(lower_x, (("col", 2),), 3, whole=True)), ((0, 0), (0, 2), (0, 0), (0, 0))
    )
    contact_pad = spread[bond_count].astype(jnp.float32)
    near_contact = window(contact_pad, 0, 0, 0, extent)

    def bond_pair(bond_index):
        shift_x, shift_y, shift_z = bond_shift(bond_index)
        weight = float(weights[bond_index])
        level_pad = spread[bond_index]
        intact = window(level_pad, 0, 0, 0, extent).astype(jnp.float32)
        prior = window(level_pad, -shift_x, -shift_y, -shift_z, extent).astype(jnp.float32)
        forward = weight * intact
        backward = weight * prior
        if nearest[bond_index] > 0.5:
            forward = forward + PENALTY * near_contact * window(
                contact_pad, shift_x, shift_y, shift_z, extent
            ) * (1.0 - intact)
            backward = backward + PENALTY * window(
                contact_pad, -shift_x, -shift_y, -shift_z, extent
            ) * near_contact * (1.0 - prior)
        forward = window(inside_pad, shift_x, shift_y, shift_z, extent) * forward
        return (forward, backward)

    diagonal = jnp.full((3,) + extent, FOUNDATION, jnp.float32)
    for bond_index in range(bond_count):
        forward, backward = bond_pair(bond_index)
        squares = np.array([entry * entry for entry in heading_of(bond_index)], np.float32)
        diagonal = diagonal + jnp.asarray(squares).reshape(3, 1, 1, 1) * (forward + backward)[None]

    def operator(vector):
        padded = rimmed(vector)
        summed = [FOUNDATION * vector[component] for component in range(3)]
        for bond_index in range(bond_count):
            shift_x, shift_y, shift_z = bond_shift(bond_index)
            forward, backward = bond_pair(bond_index)
            heading = heading_of(bond_index)
            ahead_part = heading[0] * (
                vector[0] - window(padded[0], shift_x, shift_y, shift_z, extent)
            )
            behind_part = heading[0] * (
                vector[0] - window(padded[0], -shift_x, -shift_y, -shift_z, extent)
            )
            for component in range(1, 3):
                ahead_part = ahead_part + heading[component] * (
                    vector[component] - window(padded[component], shift_x, shift_y, shift_z, extent)
                )
                behind_part = behind_part + heading[component] * (
                    vector[component]
                    - window(padded[component], -shift_x, -shift_y, -shift_z, extent)
                )
            stretch = forward * ahead_part + backward * behind_part
            for component in range(3):
                summed[component] = summed[component] + heading[component] * stretch
        return jnp.stack(summed)

    def local_means(vector):
        blocks = vector.reshape(3, cells_x * cells_y, aggregates, agg_depth)
        return (jnp.sum(blocks, axis=(1, 3)) / agg_cells).T.reshape(3 * aggregates)

    def precondition(vector, coarse):
        solved = jnp.dot(coarse_inverse, coarse, precision=lax.Precision.HIGHEST)
        spread_back = solved.reshape(aggregates, 3).T[:, None, :, None]
        scaled = (vector / diagonal).reshape(
            3, cells_x * cells_y, aggregates, agg_depth
        ) + spread_back
        return scaled.reshape(vector.shape)

    every = ("slab", "col")

    residual = rhs_force
    coarse_now = first_coarse
    direction = precondition(residual, coarse_now)
    image_vec = operator(direction)
    sums = device_rows(
        jnp.concatenate(
            [
                jnp.stack([jnp.sum(residual * direction), jnp.sum(direction * image_vec)]),
                local_means(image_vec),
            ]
        ),
        every,
    )
    rz_now = jnp.sum(sums[:, 0])
    curvature = jnp.sum(sums[:, 1])
    step_size = rz_now / curvature
    image_means = sums[:, 2:].reshape(-1)
    displacement = step_size * direction
    residual = residual - step_size * image_vec
    for iteration in range(1, ITERS):
        more = iteration + 1 < ITERS
        coarse_now = coarse_now - step_size * image_means
        precond_r = precondition(residual, coarse_now)
        image_z = operator(precond_r)
        parts = [
            jnp.stack(
                [
                    jnp.sum(residual * precond_r),
                    jnp.sum(precond_r * image_z),
                    jnp.sum(precond_r * image_vec),
                    jnp.sum(direction * image_z),
                ]
            )
        ]
        if more:
            parts.append(local_means(image_z))
        sums = device_rows(jnp.concatenate(parts), every)
        fresh_rz = jnp.sum(sums[:, 0])
        ratio = fresh_rz / rz_now
        curvature = (
            jnp.sum(sums[:, 1])
            + ratio * (jnp.sum(sums[:, 2]) + jnp.sum(sums[:, 3]))
            + ratio * ratio * curvature
        )
        rz_now = fresh_rz
        direction = precond_r + ratio * direction
        image_vec = image_z + ratio * image_vec
        step_size = rz_now / curvature
        if more:
            image_means = sums[:, 4:].reshape(-1) + ratio * image_means
        displacement = displacement + step_size * direction
        residual = residual - step_size * image_vec
    return (displacement, residual)


def solution(mesh):
    return jax.shard_map(
        on_device,
        mesh=mesh,
        in_specs=(
            P(None, "slab", "col", None),
            P(None, "slab", "col", None),
            P("slab", "col", None),
            P(("slab", "col"), None),
        ),
        out_specs=(P(None, "slab", "col", None), P(None, "slab", "col", None)),
        check_vma=False,
    )
```

```python
import jax
import jax.numpy as jnp
import numpy as np
from jax import lax
from jax.sharding import PartitionSpec as P

ITERS = 2


STIFFNESS = 0.6
PENALTY = 2.0
FOUNDATION = 1.0


def with_halo(x, sides, width, low=True, high=True):
    for axis, dim in sides:
        count, length = (lax.axis_size(axis), x.shape[dim])
        up = [(i, (i + 1) % count) for i in range(count - 1)]
        down = [(j, i) for i, j in up]
        last = lax.slice_in_dim(x, length - width, length, axis=dim)
        first = lax.slice_in_dim(x, 0, width, axis=dim)
        parts = [x]
        if low:
            parts.insert(0, lax.ppermute(last, axis, up))
        if high:
            parts.append(lax.ppermute(first, axis, down))
        x = jnp.concatenate(parts, axis=dim)
    return x


def lower_rows(levels, reach, width, flags):
    count, length = (lax.axis_size("slab"), levels.shape[1])
    up = [(i, i + 1) for i in range(count - 1)]
    down = [(j, i) for i, j in up]
    starts = [int(np.argmax(reach >= depth)) for depth in range(1, width + 1)]
    sent = jnp.concatenate(
        [levels[start:, length - depth] for depth, start in zip(range(1, width + 1), starts)]
        + [flags[length - 1 :]],
        axis=0,
    )
    got = lax.ppermute(sent, "slab", up)
    above = lax.ppermute(flags[:1], "slab", down)
    plane = levels.shape[2:]
    rows, at = ({}, 0)
    for depth, start in zip(range(1, width + 1), starts):
        size = levels.shape[0] - start
        rows[depth] = jnp.concatenate(
            [jnp.zeros((start,) + plane, levels.dtype), got[at : at + size]], axis=0
        )
        at = at + size
    below = jnp.stack([rows[depth] for depth in range(width, 0, -1)], axis=1)
    bonds = jnp.concatenate(
        [below, levels, jnp.zeros((levels.shape[0], 1) + plane, levels.dtype)], axis=1
    )
    contact_rows = jnp.concatenate(
        [jnp.zeros((width - 1,) + plane, flags.dtype), got[at:], flags, above], axis=0
    )
    return jnp.concatenate([bonds, contact_rows[None]], axis=0)


def device_rows(vector, axes):
    count = 1
    for axis in axes:
        count = count * lax.axis_size(axis)
    tiled = jnp.broadcast_to(vector[None], (count,) + vector.shape)
    return lax.all_to_all(tiled, axes, 0, 0, tiled=True)


def bond_list():
    listed = []
    for shift_x in range(-3, 4):
        for shift_y in range(-3, 4):
            for shift_z in range(-3, 4):
                radius = shift_x * shift_x + shift_y * shift_y + shift_z * shift_z
                if 0 < radius <= 9 and (shift_x, shift_y, shift_z) > (0, 0, 0):
                    listed.append((shift_x, shift_y, shift_z))
    return listed


def bond_tables():
    offsets = np.array(bond_list(), dtype=np.int32)
    lengths = np.sqrt(np.sum(offsets * offsets, axis=1).astype(np.float32)).astype(np.float32)
    unit_dirs = (offsets.astype(np.float32) / lengths[:, None]).astype(np.float32)
    weights = (np.float32(STIFFNESS) / lengths).astype(np.float32)
    nearest = (lengths < 1.5).astype(np.float32)
    return (offsets, unit_dirs, weights, nearest)


def rim_mask(count, whole, position):
    places = position * count + jnp.arange(count + 6, dtype=jnp.int32) - 3
    return ((places >= 0) & (places < whole)).astype(jnp.float32)


def window(array, shift_x, shift_y, shift_z, extent):
    return array[
        ...,
        3 + shift_x : 3 + shift_x + extent[0],
        3 + shift_y : 3 + shift_y + extent[1],
        3 + shift_z : 3 + shift_z + extent[2],
    ]


def pad_depth(array):
    return jnp.pad(array, [(0, 0)] * (array.ndim - 1) + [(3, 3)])


def on_device(rhs_force, integrity, contact, coarse_inverse):
    components, cells_x, cells_y, depth = rhs_force.shape
    bond_count = integrity.shape[0]
    aggregates = coarse_inverse.shape[0] // 3
    agg_depth = depth // aggregates
    agg_cells = cells_x * cells_y * agg_depth
    extent = (cells_x, cells_y, depth)
    offsets, unit_dirs, weights, nearest = bond_tables()
    slab_mask = rim_mask(cells_x, cells_x * lax.axis_size("slab"), lax.axis_index("slab"))
    col_mask = rim_mask(cells_y, cells_y * lax.axis_size("col"), lax.axis_index("col"))
    depth_mask = rim_mask(depth, depth, jnp.zeros((), jnp.int32))
    inside_pad = slab_mask[:, None, None] * col_mask[None, :, None] * depth_mask[None, None, :]

    def bond_shift(bond_index):
        return [int(entry) for entry in offsets[bond_index]]

    def heading_of(bond_index):
        return [float(unit_dirs[bond_index, component]) for component in range(3)]

    def rimmed(vector):
        return pad_depth(with_halo(vector, (("slab", 1), ("col", 2)), 3))

    lower_x = lower_rows(integrity, offsets[:, 0], 3, contact.astype(jnp.bfloat16))
    load_blocks = rhs_force.reshape(3, cells_x * cells_y, aggregates, agg_depth)
    load_means = (jnp.sum(load_blocks, axis=(1, 3)) / agg_cells).T.reshape(3 * aggregates)
    first_coarse = device_rows(load_means, ("slab", "col")).reshape(-1)
    first_coarse, lower_x = lax.optimization_barrier((first_coarse, lower_x))
    spread = jnp.pad(
        pad_depth(with_halo(lower_x, (("col", 2),), 3)), ((0, 0), (0, 2), (0, 0), (0, 0))
    )
    contact_pad = spread[bond_count].astype(jnp.float32)
    near_contact = window(contact_pad, 0, 0, 0, extent)

    def bond_pair(bond_index):
        shift_x, shift_y, shift_z = bond_shift(bond_index)
        weight = float(weights[bond_index])
        level_pad = spread[bond_index]
        intact = window(level_pad, 0, 0, 0, extent).astype(jnp.float32)
        prior = window(level_pad, -shift_x, -shift_y, -shift_z, extent).astype(jnp.float32)
        forward = weight * intact
        backward = weight * prior
        if nearest[bond_index] > 0.5:
            forward = forward + PENALTY * near_contact * window(
                contact_pad, shift_x, shift_y, shift_z, extent
            ) * (1.0 - intact)
            backward = backward + PENALTY * window(
                contact_pad, -shift_x, -shift_y, -shift_z, extent
            ) * near_contact * (1.0 - prior)
        forward = window(inside_pad, shift_x, shift_y, shift_z, extent) * forward
        return (forward, backward)

    diagonal = jnp.full((3,) + extent, FOUNDATION, jnp.float32)
    for bond_index in range(bond_count):
        forward, backward = bond_pair(bond_index)
        squares = np.array([entry * entry for entry in heading_of(bond_index)], np.float32)
        diagonal = diagonal + jnp.asarray(squares).reshape(3, 1, 1, 1) * (forward + backward)[None]

    def operator(vector, padded=None):
        if padded is None:
            padded = rimmed(vector)
        summed = [FOUNDATION * vector[component] for component in range(3)]
        for bond_index in range(bond_count):
            shift_x, shift_y, shift_z = bond_shift(bond_index)
            forward, backward = bond_pair(bond_index)
            heading = heading_of(bond_index)
            ahead_part = heading[0] * (
                vector[0] - window(padded[0], shift_x, shift_y, shift_z, extent)
            )
            behind_part = heading[0] * (
                vector[0] - window(padded[0], -shift_x, -shift_y, -shift_z, extent)
            )
            for component in range(1, 3):
                ahead_part = ahead_part + heading[component] * (
                    vector[component] - window(padded[component], shift_x, shift_y, shift_z, extent)
                )
                behind_part = behind_part + heading[component] * (
                    vector[component]
                    - window(padded[component], -shift_x, -shift_y, -shift_z, extent)
                )
            stretch = forward * ahead_part + backward * behind_part
            for component in range(3):
                summed[component] = summed[component] + heading[component] * stretch
        return jnp.stack(summed)

    def local_means(vector):
        blocks = vector.reshape(3, cells_x * cells_y, aggregates, agg_depth)
        return (jnp.sum(blocks, axis=(1, 3)) / agg_cells).T.reshape(3 * aggregates)

    def precondition(vector, coarse):
        solved = jnp.dot(coarse_inverse, coarse, precision=lax.Precision.HIGHEST)
        spread_back = solved.reshape(aggregates, 3).T[:, None, :, None]
        scaled = (vector / diagonal).reshape(
            3, cells_x * cells_y, aggregates, agg_depth
        ) + spread_back
        return scaled.reshape(vector.shape)

    every = ("slab", "col")

    residual = rhs_force
    coarse_now = first_coarse
    direction = precondition(residual, coarse_now)
    first_pad = rimmed(direction)
    image_vec = operator(direction, first_pad)
    image_means_local = local_means(image_vec)
    scaled_pad = rimmed(image_vec / diagonal)
    reach = jnp.dot(coarse_inverse.T, image_means_local, precision=lax.Precision.HIGHEST)
    head = 2 + image_means_local.shape[0]
    sums = device_rows(
        jnp.concatenate(
            [
                jnp.stack([jnp.sum(residual * direction), jnp.sum(direction * image_vec)]),
                image_means_local,
                reach,
            ]
        ),
        every,
    )
    rz_now = jnp.sum(sums[:, 0])
    curvature = jnp.sum(sums[:, 1])
    step_size = rz_now / curvature
    image_means = sums[:, 2:head].reshape(-1)
    solved_image = jnp.sum(sums[:, head:], axis=0).reshape(
        lax.axis_size("slab"), lax.axis_size("col"), aggregates, 3
    )
    around = lax.dynamic_slice(
        jnp.pad(solved_image, ((1, 1), (1, 1), (0, 0), (0, 0))),
        (lax.axis_index("slab"), lax.axis_index("col"), 0, 0),
        (3, 3, aggregates, 3),
    )
    around = jnp.repeat(around, np.array([3, cells_x, 3]), axis=0, total_repeat_length=cells_x + 6)
    around = jnp.repeat(around, np.array([3, cells_y, 3]), axis=1, total_repeat_length=cells_y + 6)
    around = pad_depth(jnp.repeat(around, agg_depth, axis=2).transpose(3, 0, 1, 2))
    next_pad = first_pad - step_size * (scaled_pad + around)
    displacement = step_size * direction
    residual = residual - step_size * image_vec
    for iteration in range(1, ITERS):
        more = iteration + 1 < ITERS
        coarse_now = coarse_now - step_size * image_means
        if iteration == 1:
            precond_r = window(next_pad, 0, 0, 0, extent)
            image_z = operator(precond_r, next_pad)
        else:
            precond_r = precondition(residual, coarse_now)
            image_z = operator(precond_r)
        parts = [
            jnp.stack(
                [
                    jnp.sum(residual * precond_r),
                    jnp.sum(precond_r * image_z),
                    jnp.sum(precond_r * image_vec),
                    jnp.sum(direction * image_z),
                ]
            )
        ]
        if more:
            parts.append(local_means(image_z))
        sums = device_rows(jnp.concatenate(parts), every)
        fresh_rz = jnp.sum(sums[:, 0])
        ratio = fresh_rz / rz_now
        curvature = (
            jnp.sum(sums[:, 1])
            + ratio * (jnp.sum(sums[:, 2]) + jnp.sum(sums[:, 3]))
            + ratio * ratio * curvature
        )
        rz_now = fresh_rz
        direction = precond_r + ratio * direction
        image_vec = image_z + ratio * image_vec
        step_size = rz_now / curvature
        if more:
            image_means = sums[:, 4:].reshape(-1) + ratio * image_means
        displacement = displacement + step_size * direction
        residual = residual - step_size * image_vec
    return (displacement, residual)


def solution(mesh):
    return jax.shard_map(
        on_device,
        mesh=mesh,
        in_specs=(
            P(None, "slab", "col", None),
            P(None, "slab", "col", None),
            P("slab", "col", None),
            P(("slab", "col"), None),
        ),
        out_specs=(P(None, "slab", "col", None), P(None, "slab", "col", None)),
        check_vma=False,
    )
```

```python
import jax
import jax.numpy as jnp
import numpy as np
from jax import lax
from jax.sharding import PartitionSpec as P

ITERS = 2


STIFFNESS = 0.6
PENALTY = 2.0
FOUNDATION = 1.0


def with_halo(x, sides, width, low=True, high=True):
    for axis, dim in sides:
        count, length = (lax.axis_size(axis), x.shape[dim])
        up = [(i, (i + 1) % count) for i in range(count - 1)]
        down = [(j, i) for i, j in up]
        last = lax.slice_in_dim(x, length - width, length, axis=dim)
        first = lax.slice_in_dim(x, 0, width, axis=dim)
        parts = [x]
        if low:
            parts.insert(0, lax.ppermute(last, axis, up))
        if high:
            parts.append(lax.ppermute(first, axis, down))
        x = jnp.concatenate(parts, axis=dim)
    return x


def lower_rows(levels, reach, width, flags):
    count, length = (lax.axis_size("slab"), levels.shape[1])
    up = [(i, i + 1) for i in range(count - 1)]
    down = [(j, i) for i, j in up]
    starts = [int(np.argmax(reach >= depth)) for depth in range(1, width + 1)]
    sent = jnp.concatenate(
        [levels[start:, length - depth] for depth, start in zip(range(1, width + 1), starts)]
        + [flags[length - 1 :]],
        axis=0,
    )
    got = lax.ppermute(sent, "slab", up)
    above = lax.ppermute(flags[:1], "slab", down)
    plane = levels.shape[2:]
    rows, at = ({}, 0)
    for depth, start in zip(range(1, width + 1), starts):
        size = levels.shape[0] - start
        rows[depth] = jnp.concatenate(
            [jnp.zeros((start,) + plane, levels.dtype), got[at : at + size]], axis=0
        )
        at = at + size
    below = jnp.stack([rows[depth] for depth in range(width, 0, -1)], axis=1)
    bonds = jnp.concatenate(
        [below, levels, jnp.zeros((levels.shape[0], 1) + plane, levels.dtype)], axis=1
    )
    contact_rows = jnp.concatenate(
        [jnp.zeros((width - 1,) + plane, flags.dtype), got[at:], flags, above], axis=0
    )
    return jnp.concatenate([bonds, contact_rows[None]], axis=0)


def device_rows(vector, axes):
    count = 1
    for axis in axes:
        count = count * lax.axis_size(axis)
    tiled = jnp.broadcast_to(vector[None], (count,) + vector.shape)
    return lax.all_to_all(tiled, axes, 0, 0, tiled=True)


def bond_list():
    listed = []
    for shift_x in range(-3, 4):
        for shift_y in range(-3, 4):
            for shift_z in range(-3, 4):
                radius = shift_x * shift_x + shift_y * shift_y + shift_z * shift_z
                if 0 < radius <= 9 and (shift_x, shift_y, shift_z) > (0, 0, 0):
                    listed.append((shift_x, shift_y, shift_z))
    return listed


def bond_tables():
    offsets = np.array(bond_list(), dtype=np.int32)
    lengths = np.sqrt(np.sum(offsets * offsets, axis=1).astype(np.float32)).astype(np.float32)
    unit_dirs = (offsets.astype(np.float32) / lengths[:, None]).astype(np.float32)
    weights = (np.float32(STIFFNESS) / lengths).astype(np.float32)
    nearest = (lengths < 1.5).astype(np.float32)
    return (offsets, unit_dirs, weights, nearest)


def rim_mask(count, whole, position):
    places = position * count + jnp.arange(count + 6, dtype=jnp.int32) - 3
    return ((places >= 0) & (places < whole)).astype(jnp.float32)


def window(array, shift_x, shift_y, shift_z, extent):
    return array[
        ...,
        3 + shift_x : 3 + shift_x + extent[0],
        3 + shift_y : 3 + shift_y + extent[1],
        3 + shift_z : 3 + shift_z + extent[2],
    ]


def pad_depth(array):
    return jnp.pad(array, [(0, 0)] * (array.ndim - 1) + [(3, 3)])


def on_device(rhs_force, integrity, contact, coarse_inverse):
    components, cells_x, cells_y, depth = rhs_force.shape
    bond_count = integrity.shape[0]
    aggregates = coarse_inverse.shape[0] // 3
    agg_depth = depth // aggregates
    agg_cells = cells_x * cells_y * agg_depth
    extent = (cells_x, cells_y, depth)
    offsets, unit_dirs, weights, nearest = bond_tables()
    slab_mask = rim_mask(cells_x, cells_x * lax.axis_size("slab"), lax.axis_index("slab"))
    col_mask = rim_mask(cells_y, cells_y * lax.axis_size("col"), lax.axis_index("col"))
    depth_mask = rim_mask(depth, depth, jnp.zeros((), jnp.int32))
    inside_pad = slab_mask[:, None, None] * col_mask[None, :, None] * depth_mask[None, None, :]

    def bond_shift(bond_index):
        return [int(entry) for entry in offsets[bond_index]]

    def heading_of(bond_index):
        return [float(unit_dirs[bond_index, component]) for component in range(3)]

    def rimmed(vector):
        return pad_depth(with_halo(vector, (("slab", 1), ("col", 2)), 3))

    lower_x = lower_rows(integrity, offsets[:, 0], 3, contact.astype(jnp.bfloat16))
    load_blocks = rhs_force.reshape(3, cells_x * cells_y, aggregates, agg_depth)
    load_means = (jnp.sum(load_blocks, axis=(1, 3)) / agg_cells).T.reshape(3 * aggregates)
    first_coarse = device_rows(load_means, ("slab", "col")).reshape(-1)
    first_coarse, lower_x = lax.optimization_barrier((first_coarse, lower_x))
    spread = jnp.pad(
        pad_depth(with_halo(lower_x, (("col", 2),), 3)), ((0, 0), (0, 2), (0, 0), (0, 0))
    )
    contact_pad = spread[bond_count].astype(jnp.float32)
    near_contact = window(contact_pad, 0, 0, 0, extent)

    def bond_pair(bond_index):
        shift_x, shift_y, shift_z = bond_shift(bond_index)
        weight = float(weights[bond_index])
        level_pad = spread[bond_index]
        intact = window(level_pad, 0, 0, 0, extent).astype(jnp.float32)
        prior = window(level_pad, -shift_x, -shift_y, -shift_z, extent).astype(jnp.float32)
        forward = weight * intact
        backward = weight * prior
        if nearest[bond_index] > 0.5:
            forward = forward + PENALTY * near_contact * window(
                contact_pad, shift_x, shift_y, shift_z, extent
            ) * (1.0 - intact)
            backward = backward + PENALTY * window(
                contact_pad, -shift_x, -shift_y, -shift_z, extent
            ) * near_contact * (1.0 - prior)
        forward = window(inside_pad, shift_x, shift_y, shift_z, extent) * forward
        return (forward, backward)

    diagonal = jnp.full((3,) + extent, FOUNDATION, jnp.float32)
    for bond_index in range(bond_count):
        forward, backward = bond_pair(bond_index)
        squares = np.array([entry * entry for entry in heading_of(bond_index)], np.float32)
        diagonal = diagonal + jnp.asarray(squares).reshape(3, 1, 1, 1) * (forward + backward)[None]

    def operator(vector, padded=None):
        if padded is None:
            padded = rimmed(vector)
        summed = [FOUNDATION * vector[component] for component in range(3)]
        for bond_index in range(bond_count):
            shift_x, shift_y, shift_z = bond_shift(bond_index)
            forward, backward = bond_pair(bond_index)
            heading = heading_of(bond_index)
            ahead_part = heading[0] * (
                vector[0] - window(padded[0], shift_x, shift_y, shift_z, extent)
            )
            behind_part = heading[0] * (
                vector[0] - window(padded[0], -shift_x, -shift_y, -shift_z, extent)
            )
            for component in range(1, 3):
                ahead_part = ahead_part + heading[component] * (
                    vector[component] - window(padded[component], shift_x, shift_y, shift_z, extent)
                )
                behind_part = behind_part + heading[component] * (
                    vector[component]
                    - window(padded[component], -shift_x, -shift_y, -shift_z, extent)
                )
            stretch = forward * ahead_part + backward * behind_part
            for component in range(3):
                summed[component] = summed[component] + heading[component] * stretch
        return jnp.stack(summed)

    def local_means(vector):
        blocks = vector.reshape(3, cells_x * cells_y, aggregates, agg_depth)
        return (jnp.sum(blocks, axis=(1, 3)) / agg_cells).T.reshape(3 * aggregates)

    def precondition(vector, coarse):
        solved = jnp.dot(coarse_inverse, coarse, precision=lax.Precision.HIGHEST)
        spread_back = solved.reshape(aggregates, 3).T[:, None, :, None]
        scaled = (vector / diagonal).reshape(
            3, cells_x * cells_y, aggregates, agg_depth
        ) + spread_back
        return scaled.reshape(vector.shape)

    every = ("slab", "col")

    residual = rhs_force
    coarse_now = first_coarse
    direction = precondition(residual, coarse_now)
    first_pad = rimmed(direction)
    image_vec = operator(direction, first_pad)
    image_means_local = local_means(image_vec)
    scaled_pad = rimmed(image_vec / diagonal)
    reach = lax.dot_general(
        image_means_local, coarse_inverse, (((0,), (0,)), ((), ())), precision=lax.Precision.HIGHEST
    )
    head = 2 + image_means_local.shape[0]
    sums = device_rows(
        jnp.concatenate(
            [
                jnp.stack([jnp.sum(residual * direction), jnp.sum(direction * image_vec)]),
                image_means_local,
                reach,
            ]
        ),
        every,
    )
    rz_now = jnp.sum(sums[:, 0])
    curvature = jnp.sum(sums[:, 1])
    step_size = rz_now / curvature
    image_means = sums[:, 2:head].reshape(-1)
    solved_image = jnp.sum(sums[:, head:], axis=0).reshape(
        lax.axis_size("slab"), lax.axis_size("col"), aggregates, 3
    )
    around = lax.dynamic_slice(
        jnp.pad(solved_image, ((1, 1), (1, 1), (0, 0), (0, 0))),
        (lax.axis_index("slab"), lax.axis_index("col"), 0, 0),
        (3, 3, aggregates, 3),
    )
    around = jnp.repeat(around, np.array([3, cells_x, 3]), axis=0, total_repeat_length=cells_x + 6)
    around = jnp.repeat(around, np.array([3, cells_y, 3]), axis=1, total_repeat_length=cells_y + 6)
    around = pad_depth(jnp.repeat(around, agg_depth, axis=2).transpose(3, 0, 1, 2))
    next_pad = first_pad - step_size * (scaled_pad + around)
    displacement = step_size * direction
    residual = residual - step_size * image_vec
    for iteration in range(1, ITERS):
        more = iteration + 1 < ITERS
        coarse_now = coarse_now - step_size * image_means
        if iteration == 1:
            precond_r = window(next_pad, 0, 0, 0, extent)
            image_z = operator(precond_r, next_pad)
        else:
            precond_r = precondition(residual, coarse_now)
            image_z = operator(precond_r)
        parts = [
            jnp.stack(
                [
                    jnp.sum(residual * precond_r),
                    jnp.sum(precond_r * image_z),
                    jnp.sum(precond_r * image_vec),
                    jnp.sum(direction * image_z),
                ]
            )
        ]
        if more:
            parts.append(local_means(image_z))
        sums = device_rows(jnp.concatenate(parts), every)
        fresh_rz = jnp.sum(sums[:, 0])
        ratio = fresh_rz / rz_now
        curvature = (
            jnp.sum(sums[:, 1])
            + ratio * (jnp.sum(sums[:, 2]) + jnp.sum(sums[:, 3]))
            + ratio * ratio * curvature
        )
        rz_now = fresh_rz
        direction = precond_r + ratio * direction
        image_vec = image_z + ratio * image_vec
        step_size = rz_now / curvature
        if more:
            image_means = sums[:, 4:].reshape(-1) + ratio * image_means
        displacement = displacement + step_size * direction
        residual = residual - step_size * image_vec
    return (displacement, residual)


def solution(mesh):
    return jax.shard_map(
        on_device,
        mesh=mesh,
        in_specs=(
            P(None, "slab", "col", None),
            P(None, "slab", "col", None),
            P("slab", "col", None),
            P(("slab", "col"), None),
        ),
        out_specs=(P(None, "slab", "col", None), P(None, "slab", "col", None)),
        check_vma=False,
    )
```

```python
import jax
import jax.numpy as jnp
import numpy as np
from jax import lax
from jax.sharding import PartitionSpec as P

ITERS = 2


STIFFNESS = 0.6
PENALTY = 2.0
FOUNDATION = 1.0


def with_halo(x, sides, width, low=True, high=True):
    for axis, dim in sides:
        count, length = (lax.axis_size(axis), x.shape[dim])
        up = [(i, (i + 1) % count) for i in range(count - 1)]
        down = [(j, i) for i, j in up]
        last = lax.slice_in_dim(x, length - width, length, axis=dim)
        first = lax.slice_in_dim(x, 0, width, axis=dim)
        parts = [x]
        if low:
            parts.insert(0, lax.ppermute(last, axis, up))
        if high:
            parts.append(lax.ppermute(first, axis, down))
        x = jnp.concatenate(parts, axis=dim)
    return x


def lower_rows(levels, reach, width, flags):
    count, length = (lax.axis_size("slab"), levels.shape[1])
    up = [(i, i + 1) for i in range(count - 1)]
    down = [(j, i) for i, j in up]
    starts = [int(np.argmax(reach >= depth)) for depth in range(1, width + 1)]
    sent = jnp.concatenate(
        [levels[start:, length - depth] for depth, start in zip(range(1, width + 1), starts)]
        + [flags[length - 1 :]],
        axis=0,
    )
    got = lax.ppermute(sent, "slab", up)
    above = lax.ppermute(flags[:1], "slab", down)
    plane = levels.shape[2:]
    rows, at = ({}, 0)
    for depth, start in zip(range(1, width + 1), starts):
        size = levels.shape[0] - start
        rows[depth] = jnp.concatenate(
            [jnp.zeros((start,) + plane, levels.dtype), got[at : at + size]], axis=0
        )
        at = at + size
    below = jnp.stack([rows[depth] for depth in range(width, 0, -1)], axis=1)
    bonds = jnp.concatenate(
        [below, levels, jnp.zeros((levels.shape[0], 1) + plane, levels.dtype)], axis=1
    )
    contact_rows = jnp.concatenate(
        [jnp.zeros((width - 1,) + plane, flags.dtype), got[at:], flags, above], axis=0
    )
    return jnp.concatenate([bonds, contact_rows[None]], axis=0)


def device_rows(vector, axes):
    count = 1
    for axis in axes:
        count = count * lax.axis_size(axis)
    tiled = jnp.broadcast_to(vector[None], (count,) + vector.shape)
    return lax.all_to_all(tiled, axes, 0, 0, tiled=True)


def bond_list():
    listed = []
    for shift_x in range(-3, 4):
        for shift_y in range(-3, 4):
            for shift_z in range(-3, 4):
                radius = shift_x * shift_x + shift_y * shift_y + shift_z * shift_z
                if 0 < radius <= 9 and (shift_x, shift_y, shift_z) > (0, 0, 0):
                    listed.append((shift_x, shift_y, shift_z))
    return listed


def bond_tables():
    offsets = np.array(bond_list(), dtype=np.int32)
    lengths = np.sqrt(np.sum(offsets * offsets, axis=1).astype(np.float32)).astype(np.float32)
    unit_dirs = (offsets.astype(np.float32) / lengths[:, None]).astype(np.float32)
    weights = (np.float32(STIFFNESS) / lengths).astype(np.float32)
    nearest = (lengths < 1.5).astype(np.float32)
    return (offsets, unit_dirs, weights, nearest)


def rim_mask(count, whole, position):
    places = position * count + jnp.arange(count + 6, dtype=jnp.int32) - 3
    return ((places >= 0) & (places < whole)).astype(jnp.float32)


def window(array, shift_x, shift_y, shift_z, extent):
    return array[
        ...,
        3 + shift_x : 3 + shift_x + extent[0],
        3 + shift_y : 3 + shift_y + extent[1],
        3 + shift_z : 3 + shift_z + extent[2],
    ]


def pad_depth(array):
    return jnp.pad(array, [(0, 0)] * (array.ndim - 1) + [(3, 3)])


def on_device(rhs_force, integrity, contact, coarse_inverse):
    components, cells_x, cells_y, depth = rhs_force.shape
    bond_count = integrity.shape[0]
    aggregates = coarse_inverse.shape[0] // 3
    agg_depth = depth // aggregates
    agg_cells = cells_x * cells_y * agg_depth
    extent = (cells_x, cells_y, depth)
    offsets, unit_dirs, weights, nearest = bond_tables()
    slab_mask = rim_mask(cells_x, cells_x * lax.axis_size("slab"), lax.axis_index("slab"))
    col_mask = rim_mask(cells_y, cells_y * lax.axis_size("col"), lax.axis_index("col"))
    depth_mask = rim_mask(depth, depth, jnp.zeros((), jnp.int32))
    inside_pad = slab_mask[:, None, None] * col_mask[None, :, None] * depth_mask[None, None, :]

    def bond_shift(bond_index):
        return [int(entry) for entry in offsets[bond_index]]

    def heading_of(bond_index):
        return [float(unit_dirs[bond_index, component]) for component in range(3)]

    def rimmed(vector):
        return pad_depth(with_halo(vector, (("slab", 1), ("col", 2)), 3))

    lower_x = lower_rows(integrity, offsets[:, 0], 3, contact.astype(jnp.bfloat16))
    load_blocks = rhs_force.reshape(3, cells_x * cells_y, aggregates, agg_depth)
    load_means = (jnp.sum(load_blocks, axis=(1, 3)) / agg_cells).T.reshape(3 * aggregates)
    first_coarse = device_rows(load_means, ("slab", "col")).reshape(-1)
    first_coarse, lower_x = lax.optimization_barrier((first_coarse, lower_x))
    spread = jnp.pad(
        pad_depth(with_halo(lower_x, (("col", 2),), 3)), ((0, 0), (0, 2), (0, 0), (0, 0))
    )
    contact_pad = spread[bond_count].astype(jnp.float32)
    near_contact = contact.astype(jnp.float32)

    def bond_pair(bond_index):
        shift_x, shift_y, shift_z = bond_shift(bond_index)
        weight = float(weights[bond_index])
        level_pad = spread[bond_index]
        intact = integrity[bond_index].astype(jnp.float32)
        prior = window(level_pad, -shift_x, -shift_y, -shift_z, extent).astype(jnp.float32)
        forward = weight * intact
        backward = weight * prior
        if nearest[bond_index] > 0.5:
            forward = forward + PENALTY * near_contact * window(
                contact_pad, shift_x, shift_y, shift_z, extent
            ) * (1.0 - intact)
            backward = backward + PENALTY * window(
                contact_pad, -shift_x, -shift_y, -shift_z, extent
            ) * near_contact * (1.0 - prior)
        forward = window(inside_pad, shift_x, shift_y, shift_z, extent) * forward
        return (forward, backward)

    diagonal = jnp.full((3,) + extent, FOUNDATION, jnp.float32)
    for bond_index in range(bond_count):
        forward, backward = bond_pair(bond_index)
        squares = np.array([entry * entry for entry in heading_of(bond_index)], np.float32)
        diagonal = diagonal + jnp.asarray(squares).reshape(3, 1, 1, 1) * (forward + backward)[None]

    def operator(vector):
        padded = rimmed(vector)
        summed = [FOUNDATION * vector[component] for component in range(3)]
        for bond_index in range(bond_count):
            shift_x, shift_y, shift_z = bond_shift(bond_index)
            forward, backward = bond_pair(bond_index)
            heading = heading_of(bond_index)
            ahead_part = heading[0] * (
                vector[0] - window(padded[0], shift_x, shift_y, shift_z, extent)
            )
            behind_part = heading[0] * (
                vector[0] - window(padded[0], -shift_x, -shift_y, -shift_z, extent)
            )
            for component in range(1, 3):
                ahead_part = ahead_part + heading[component] * (
                    vector[component] - window(padded[component], shift_x, shift_y, shift_z, extent)
                )
                behind_part = behind_part + heading[component] * (
                    vector[component]
                    - window(padded[component], -shift_x, -shift_y, -shift_z, extent)
                )
            stretch = forward * ahead_part + backward * behind_part
            for component in range(3):
                summed[component] = summed[component] + heading[component] * stretch
        return jnp.stack(summed)

    def local_means(vector):
        blocks = vector.reshape(3, cells_x * cells_y, aggregates, agg_depth)
        return (jnp.sum(blocks, axis=(1, 3)) / agg_cells).T.reshape(3 * aggregates)

    def precondition(vector, coarse):
        solved = jnp.dot(coarse_inverse, coarse, precision=lax.Precision.HIGHEST)
        spread_back = solved.reshape(aggregates, 3).T[:, None, :, None]
        scaled = (vector / diagonal).reshape(
            3, cells_x * cells_y, aggregates, agg_depth
        ) + spread_back
        return scaled.reshape(vector.shape)

    every = ("slab", "col")

    residual = rhs_force
    coarse_now = first_coarse
    direction = precondition(residual, coarse_now)
    image_vec = operator(direction)
    sums = device_rows(
        jnp.concatenate(
            [
                jnp.stack([jnp.sum(residual * direction), jnp.sum(direction * image_vec)]),
                local_means(image_vec),
            ]
        ),
        every,
    )
    rz_now = jnp.sum(sums[:, 0])
    curvature = jnp.sum(sums[:, 1])
    step_size = rz_now / curvature
    image_means = sums[:, 2:].reshape(-1)
    displacement = step_size * direction
    residual = residual - step_size * image_vec
    for iteration in range(1, ITERS):
        more = iteration + 1 < ITERS
        coarse_now = coarse_now - step_size * image_means
        precond_r = precondition(residual, coarse_now)
        image_z = operator(precond_r)
        parts = [
            jnp.stack(
                [
                    jnp.sum(residual * precond_r),
                    jnp.sum(precond_r * image_z),
                    jnp.sum(precond_r * image_vec),
                    jnp.sum(direction * image_z),
                ]
            )
        ]
        if more:
            parts.append(local_means(image_z))
        sums = device_rows(jnp.concatenate(parts), every)
        fresh_rz = jnp.sum(sums[:, 0])
        ratio = fresh_rz / rz_now
        curvature = (
            jnp.sum(sums[:, 1])
            + ratio * (jnp.sum(sums[:, 2]) + jnp.sum(sums[:, 3]))
            + ratio * ratio * curvature
        )
        rz_now = fresh_rz
        direction = precond_r + ratio * direction
        image_vec = image_z + ratio * image_vec
        step_size = rz_now / curvature
        if more:
            image_means = sums[:, 4:].reshape(-1) + ratio * image_means
        displacement = displacement + step_size * direction
        residual = residual - step_size * image_vec
    return (displacement, residual)


def solution(mesh):
    return jax.shard_map(
        on_device,
        mesh=mesh,
        in_specs=(
            P(None, "slab", "col", None),
            P(None, "slab", "col", None),
            P("slab", "col", None),
            P(("slab", "col"), None),
        ),
        out_specs=(P(None, "slab", "col", None), P(None, "slab", "col", None)),
        check_vma=False,
    )
```

```python
import jax
import jax.numpy as jnp
import numpy as np
from jax import lax
from jax.sharding import PartitionSpec as P

ITERS = 2


STIFFNESS = 0.6
PENALTY = 2.0
FOUNDATION = 1.0


def with_halo(x, sides, width, low=True, high=True):
    for axis, dim in sides:
        count, length = (lax.axis_size(axis), x.shape[dim])
        up = [(i, (i + 1) % count) for i in range(count - 1)]
        down = [(j, i) for i, j in up]
        last = lax.slice_in_dim(x, length - width, length, axis=dim)
        first = lax.slice_in_dim(x, 0, width, axis=dim)
        parts = [x]
        if low:
            parts.insert(0, lax.ppermute(last, axis, up))
        if high:
            parts.append(lax.ppermute(first, axis, down))
        x = jnp.concatenate(parts, axis=dim)
    return x


def lower_rows(levels, reach, width, flags):
    count, length = (lax.axis_size("slab"), levels.shape[1])
    up = [(i, i + 1) for i in range(count - 1)]
    down = [(j, i) for i, j in up]
    starts = [int(np.argmax(reach >= depth)) for depth in range(1, width + 1)]
    sent = jnp.concatenate(
        [levels[start:, length - depth] for depth, start in zip(range(1, width + 1), starts)]
        + [flags[length - 1 :]],
        axis=0,
    )
    got = lax.ppermute(sent, "slab", up)
    above = lax.ppermute(flags[:1], "slab", down)
    plane = levels.shape[2:]
    rows, at = ({}, 0)
    for depth, start in zip(range(1, width + 1), starts):
        size = levels.shape[0] - start
        rows[depth] = jnp.concatenate(
            [jnp.zeros((start,) + plane, levels.dtype), got[at : at + size]], axis=0
        )
        at = at + size
    below = jnp.stack([rows[depth] for depth in range(width, 0, -1)], axis=1)
    bonds = jnp.concatenate(
        [below, levels, jnp.zeros((levels.shape[0], 1) + plane, levels.dtype)], axis=1
    )
    contact_rows = jnp.concatenate(
        [jnp.zeros((width - 1,) + plane, flags.dtype), got[at:], flags, above], axis=0
    )
    return jnp.concatenate([bonds, contact_rows[None]], axis=0)


def device_rows(vector, axes):
    count = 1
    for axis in axes:
        count = count * lax.axis_size(axis)
    tiled = jnp.broadcast_to(vector[None], (count,) + vector.shape)
    return lax.all_to_all(tiled, axes, 0, 0, tiled=True)


def bond_list():
    listed = []
    for shift_x in range(-3, 4):
        for shift_y in range(-3, 4):
            for shift_z in range(-3, 4):
                radius = shift_x * shift_x + shift_y * shift_y + shift_z * shift_z
                if 0 < radius <= 9 and (shift_x, shift_y, shift_z) > (0, 0, 0):
                    listed.append((shift_x, shift_y, shift_z))
    return listed


def bond_tables():
    offsets = np.array(bond_list(), dtype=np.int32)
    lengths = np.sqrt(np.sum(offsets * offsets, axis=1).astype(np.float32)).astype(np.float32)
    unit_dirs = (offsets.astype(np.float32) / lengths[:, None]).astype(np.float32)
    weights = (np.float32(STIFFNESS) / lengths).astype(np.float32)
    nearest = (lengths < 1.5).astype(np.float32)
    return (offsets, unit_dirs, weights, nearest)


def rim_mask(count, whole, position):
    places = position * count + jnp.arange(count + 6, dtype=jnp.int32) - 3
    return ((places >= 0) & (places < whole)).astype(jnp.float32)


def window(array, shift_x, shift_y, shift_z, extent):
    return array[
        ...,
        3 + shift_x : 3 + shift_x + extent[0],
        3 + shift_y : 3 + shift_y + extent[1],
        3 + shift_z : 3 + shift_z + extent[2],
    ]


def pad_depth(array):
    return jnp.pad(array, [(0, 0)] * (array.ndim - 1) + [(3, 3)])


def on_device(rhs_force, integrity, contact, coarse_inverse):
    components, cells_x, cells_y, depth = rhs_force.shape
    bond_count = integrity.shape[0]
    aggregates = coarse_inverse.shape[0] // 3
    agg_depth = depth // aggregates
    agg_cells = cells_x * cells_y * agg_depth
    extent = (cells_x, cells_y, depth)
    offsets, unit_dirs, weights, nearest = bond_tables()
    slab_mask = rim_mask(cells_x, cells_x * lax.axis_size("slab"), lax.axis_index("slab"))
    col_mask = rim_mask(cells_y, cells_y * lax.axis_size("col"), lax.axis_index("col"))
    depth_mask = rim_mask(depth, depth, jnp.zeros((), jnp.int32))
    inside_pad = slab_mask[:, None, None] * col_mask[None, :, None] * depth_mask[None, None, :]

    def bond_shift(bond_index):
        return [int(entry) for entry in offsets[bond_index]]

    def heading_of(bond_index):
        return [float(unit_dirs[bond_index, component]) for component in range(3)]

    def rimmed(vector):
        return pad_depth(with_halo(vector, (("slab", 1), ("col", 2)), 3))

    lower_x = lower_rows(integrity, offsets[:, 0], 3, contact.astype(jnp.bfloat16))
    load_blocks = rhs_force.reshape(3, cells_x * cells_y, aggregates, agg_depth)
    load_means = (jnp.sum(load_blocks, axis=(1, 3)) / agg_cells).T.reshape(3 * aggregates)
    first_coarse = device_rows(load_means, ("slab", "col")).reshape(-1)
    first_coarse, lower_x = lax.optimization_barrier((first_coarse, lower_x))
    spread = jnp.pad(
        pad_depth(with_halo(lower_x, (("col", 2),), 3)), ((0, 0), (0, 2), (0, 0), (0, 0))
    )
    contact_pad = spread[bond_count].astype(jnp.float32)
    near_contact = contact.astype(jnp.float32)

    def bond_pair(bond_index):
        shift_x, shift_y, shift_z = bond_shift(bond_index)
        weight = float(weights[bond_index])
        level_pad = spread[bond_index]
        intact = integrity[bond_index].astype(jnp.float32)
        prior = window(level_pad, -shift_x, -shift_y, -shift_z, extent).astype(jnp.float32)
        forward = weight * intact
        backward = weight * prior
        if nearest[bond_index] > 0.5:
            forward = forward + PENALTY * near_contact * window(
                contact_pad, shift_x, shift_y, shift_z, extent
            ) * (1.0 - intact)
            backward = backward + PENALTY * window(
                contact_pad, -shift_x, -shift_y, -shift_z, extent
            ) * near_contact * (1.0 - prior)
        forward = (
            slab_mask[3 + shift_x : 3 + shift_x + extent[0], None, None]
            * col_mask[None, 3 + shift_y : 3 + shift_y + extent[1], None]
            * depth_mask[None, None, 3 + shift_z : 3 + shift_z + extent[2]]
        ) * forward
        return (forward, backward)

    diagonal = jnp.full((3,) + extent, FOUNDATION, jnp.float32)
    for bond_index in range(bond_count):
        forward, backward = bond_pair(bond_index)
        squares = np.array([entry * entry for entry in heading_of(bond_index)], np.float32)
        diagonal = diagonal + jnp.asarray(squares).reshape(3, 1, 1, 1) * (forward + backward)[None]

    def operator(vector):
        padded = rimmed(vector)
        summed = [FOUNDATION * vector[component] for component in range(3)]
        for bond_index in range(bond_count):
            shift_x, shift_y, shift_z = bond_shift(bond_index)
            forward, backward = bond_pair(bond_index)
            heading = heading_of(bond_index)
            ahead_part = heading[0] * (
                vector[0] - window(padded[0], shift_x, shift_y, shift_z, extent)
            )
            behind_part = heading[0] * (
                vector[0] - window(padded[0], -shift_x, -shift_y, -shift_z, extent)
            )
            for component in range(1, 3):
                ahead_part = ahead_part + heading[component] * (
                    vector[component] - window(padded[component], shift_x, shift_y, shift_z, extent)
                )
                behind_part = behind_part + heading[component] * (
                    vector[component]
                    - window(padded[component], -shift_x, -shift_y, -shift_z, extent)
                )
            stretch = forward * ahead_part + backward * behind_part
            for component in range(3):
                summed[component] = summed[component] + heading[component] * stretch
        return jnp.stack(summed)

    def local_means(vector):
        blocks = vector.reshape(3, cells_x * cells_y, aggregates, agg_depth)
        return (jnp.sum(blocks, axis=(1, 3)) / agg_cells).T.reshape(3 * aggregates)

    def precondition(vector, coarse):
        solved = jnp.dot(coarse_inverse, coarse, precision=lax.Precision.HIGHEST)
        spread_back = solved.reshape(aggregates, 3).T[:, None, :, None]
        scaled = (vector / diagonal).reshape(
            3, cells_x * cells_y, aggregates, agg_depth
        ) + spread_back
        return scaled.reshape(vector.shape)

    every = ("slab", "col")

    residual = rhs_force
    coarse_now = first_coarse
    direction = precondition(residual, coarse_now)
    image_vec = operator(direction)
    sums = device_rows(
        jnp.concatenate(
            [
                jnp.stack([jnp.sum(residual * direction), jnp.sum(direction * image_vec)]),
                local_means(image_vec),
            ]
        ),
        every,
    )
    rz_now = jnp.sum(sums[:, 0])
    curvature = jnp.sum(sums[:, 1])
    step_size = rz_now / curvature
    image_means = sums[:, 2:].reshape(-1)
    displacement = step_size * direction
    residual = residual - step_size * image_vec
    for iteration in range(1, ITERS):
        more = iteration + 1 < ITERS
        coarse_now = coarse_now - step_size * image_means
        precond_r = precondition(residual, coarse_now)
        image_z = operator(precond_r)
        parts = [
            jnp.stack(
                [
                    jnp.sum(residual * precond_r),
                    jnp.sum(precond_r * image_z),
                    jnp.sum(precond_r * image_vec),
                    jnp.sum(direction * image_z),
                ]
            )
        ]
        if more:
            parts.append(local_means(image_z))
        sums = device_rows(jnp.concatenate(parts), every)
        fresh_rz = jnp.sum(sums[:, 0])
        ratio = fresh_rz / rz_now
        curvature = (
            jnp.sum(sums[:, 1])
            + ratio * (jnp.sum(sums[:, 2]) + jnp.sum(sums[:, 3]))
            + ratio * ratio * curvature
        )
        rz_now = fresh_rz
        direction = precond_r + ratio * direction
        image_vec = image_z + ratio * image_vec
        step_size = rz_now / curvature
        if more:
            image_means = sums[:, 4:].reshape(-1) + ratio * image_means
        displacement = displacement + step_size * direction
        residual = residual - step_size * image_vec
    return (displacement, residual)


def solution(mesh):
    return jax.shard_map(
        on_device,
        mesh=mesh,
        in_specs=(
            P(None, "slab", "col", None),
            P(None, "slab", "col", None),
            P("slab", "col", None),
            P(("slab", "col"), None),
        ),
        out_specs=(P(None, "slab", "col", None), P(None, "slab", "col", None)),
        check_vma=False,
    )
```
